32 devices in a mesh: groups: 2 (over y), sta: 4 (over z), band: 2 (over x), seg: 2 (over core).
Axes of the slice: x: 2, y: 2, z: 4, core: 2. Of those that a mesh axis runs over, the one named last changes fastest.
Arguments:
- spectra: float32 [8, 2, 512, 1024], P('seg', None, 'band', ('groups', 'sta')), parts along dimension 3, may hold values from -600 to 600, as said below
- plan: int32 [4], P('groups'), parts along dimension 0, may hold values from 0 to 3
- pair_mask: int32 [8, 4], P('groups'), parts along dimension 0, may hold values 0 or 1
Outputs:
- correlations: bfloat16 [2, 256, 128, 1024], P(None, 'band', 'seg', ('groups', 'sta')), parts along dimension 3
The draws below stay inside these ranges and needn't reach their ends.
There are 2 independent parts, one for each index of `groups`. The reference program is written for one: setup_inputs(seed, part) draws one part's arguments, and reference() takes and returns one part's arrays. A program takes and returns all parts, laid end to end along the dimension named above; each array names one. Nothing has to cross between parts.
Inputs may be any that keep to these rules, and one draw needn't show every extreme that they name: spectra of the station records, real part first and imaginary part second.
All inputs are finite; a program needn't handle non-finite values.
Results may differ from the reference program's by a relative error of at most 0.0072.
Values may be sent and summed in bfloat16 or wider, within the bound.
No kernel may reach another device: no remote copies, remote signals or barrier semaphores. Data moves between devices by JAX's collectives and lax.ppermute only.
A program may use at most 128 MiB of HBM per device.

```python
import math
import jax
import jax.numpy as jnp
from jax import lax

SEGS = 8
STEPS = 2
SRC = 128
BAND_BINS = 256
HALF = 64
LAGS = 128
STATIONS = 512
NBLK = 4
BINS = 512
N_BAND = 2


def draw_spectra(key, part):
    keys = jax.random.split(jax.random.fold_in(key, 11), 4)
    shape = (SEGS, 2, BINS, STATIONS)
    base = jnp.clip(jax.random.normal(keys[0], shape, jnp.float32), -6.0, 6.0)
    station = jnp.exp(jax.random.uniform(keys[1], (1, 1, 1, STATIONS), jnp.float32, 0.0, math.log(10.0)))
    knot_count = BINS // BAND_BINS + 1
    knot_logs = jax.random.uniform(keys[2], (knot_count,), jnp.float32, math.log(0.2), math.log(5.0))
    bin_index = jnp.arange(BINS, dtype=jnp.int32)
    lower_knot = bin_index // BAND_BINS
    fraction = (bin_index % BAND_BINS).astype(jnp.float32) / BAND_BINS
    log_envelope = knot_logs[lower_knot] * (1.0 - fraction) + knot_logs[lower_knot + 1] * fraction
    envelope = jnp.exp(log_envelope).reshape(1, 1, BINS, 1)
    segment = jnp.exp(jax.random.uniform(keys[3], (SEGS, 1, 1, 1), jnp.float32, math.log(0.5), math.log(2.0)))
    return (base * station * envelope * segment).astype(jnp.float32)


def touch_ends(result, key, smallest, high):
    longest = result.shape.index(max(result.shape))
    spots = []
    for shift in (0, 1):
        where = [jax.random.randint(jax.random.fold_in(key, axis), (), 0, length) for axis, length in enumerate(result.shape)]
        where[longest] = (where[longest] + shift) % result.shape[longest]
        spots.append(tuple(where))
    return result.at[spots[0]].set(smallest).at[spots[1]].set(high)


def setup_inputs(seed: int = 0, part: int = 0) -> dict:
    arg_keys = jax.random.split(jax.random.key(seed), 4)
    own_keys = jax.random.split(jax.random.fold_in(arg_keys[3], part), 4)
    spectra = draw_spectra(jax.random.fold_in(jax.random.fold_in(arg_keys[3], part), 71), part)
    plan = jax.random.randint(own_keys[1], (STEPS,), 0, NBLK).astype(jnp.int32)
    pair_mask = touch_ends((jax.random.randint(own_keys[2], (NBLK, NBLK), 0, 4) < 3).astype(jnp.int32), jax.random.fold_in(own_keys[2], 1), 0, 1)
    return {"spectra": spectra, "plan": plan, "pair_mask": pair_mask}


EPSILON = 1e-06

def whiten(spectra):
    amplitude = jnp.sqrt(spectra[:, 0] ** 2 + spectra[:, 1] ** 2)
    extended = jnp.pad(amplitude, ((0, 0), (HALF + 1, HALF), (0, 0)))
    running = jnp.cumsum(extended, axis=1)
    window_sums = running[:, 2 * HALF + 1:] - running[:, :BINS]
    bin_number = jnp.arange(BINS, dtype=jnp.int32)
    in_range = (jnp.minimum(bin_number + HALF, BINS - 1) - jnp.maximum(bin_number - HALF, 0) + 1).astype(jnp.float32)
    smooth = window_sums / in_range[None, :, None]
    return (spectra / (smooth[:, None] + EPSILON)).astype(jnp.bfloat16)

def lag_table(first_bin):
    bin_number = first_bin + jnp.arange(BAND_BINS, dtype=jnp.int32)
    lag_number = jnp.arange(LAGS, dtype=jnp.int32) - LAGS // 2
    phase_steps = jnp.remainder(lag_number[:, None] * bin_number[None, :], 2 * BAND_BINS)
    phases = phase_steps.astype(jnp.float32) * (math.pi / BAND_BINS)
    normalizer = 1.0 / math.sqrt(SEGS * BAND_BINS)
    weights = jnp.stack([jnp.cos(phases), -jnp.sin(phases)], axis=2) * normalizer
    return weights.astype(jnp.bfloat16).reshape(LAGS, 2 * BAND_BINS)

def cross_terms(sources, receivers):
    src_real = sources[:, 0].astype(jnp.float32)
    src_imag = sources[:, 1].astype(jnp.float32)
    left_stack = jnp.stack([jnp.concatenate([src_real, src_imag], 0), jnp.concatenate([src_imag, -src_real], 0)], 0)
    right_stack = jnp.concatenate([receivers[:, 0], receivers[:, 1]], 0).astype(jnp.float32)
    cross_spectra = jnp.einsum('ctfs,tfn->fcsn', left_stack, right_stack, precision=lax.Precision.HIGHEST)
    width_src = sources.shape[3]
    width_rec = receivers.shape[3]
    return cross_spectra.astype(jnp.bfloat16).reshape(2 * BAND_BINS, width_src * width_rec)

def reference(spectra, plan, pair_mask):
    white = whiten(spectra)
    results = []
    for step_number in range(STEPS):
        block_number = plan[step_number]
        sources = lax.dynamic_slice_in_dim(white, (block_number * SRC).astype(jnp.int32), SRC, 3)
        source_ids = block_number * SRC + jnp.arange(SRC, dtype=jnp.int32)
        bands = []
        for band_number in range(N_BAND):
            lowest = band_number * BAND_BINS
            lag_weights = lag_table(lowest)
            source_band = sources[:, :, lowest:lowest + BAND_BINS]
            white_band = white[:, :, lowest:lowest + BAND_BINS]

            def receiver_block(receiver_number):
                receivers = lax.dynamic_slice_in_dim(white_band, (receiver_number * SRC).astype(jnp.int32), SRC, 3)
                cross_spectra = cross_terms(source_band, receivers)
                correlated = jnp.dot(lag_weights, cross_spectra, preferred_element_type=jnp.float32).reshape(LAGS, SRC, SRC)
                receiver_ids = receiver_number * SRC + jnp.arange(SRC, dtype=jnp.int32)
                keep_pairs = (source_ids[:, None] != receiver_ids[None, :]).astype(jnp.float32)
                keep_pairs = keep_pairs * pair_mask[block_number, receiver_number].astype(jnp.float32)
                return (correlated * keep_pairs[None]).astype(jnp.bfloat16)
            stacked = lax.map(receiver_block, jnp.arange(NBLK, dtype=jnp.int32))
            bands.append(jnp.moveaxis(stacked, 0, 2).reshape(LAGS, SRC, STATIONS))
        results.append(jnp.concatenate(bands, 0))
    return jnp.stack(results, 0)
```

```python
import math

import jax
import jax.numpy as jnp
from jax import lax
from jax.sharding import PartitionSpec as P

SEGS = 8
STEPS = 2
SRC = 128
BLK_DEV = 1
BAND_BINS = 256
HALF = 64
LAGS = 128


EPSILON = 1e-06


def padded(cells, sides, width):
    for axis, dim in sides:
        count = lax.axis_size(axis)
        ends = count - 1
        head = lax.slice_in_dim(cells, 0, width, axis=dim)
        tail = lax.slice_in_dim(cells, cells.shape[dim] - width, cells.shape[dim], axis=dim)
        cells = jnp.concatenate(
            [
                lax.ppermute(tail, axis, [(i, (i + 1) % count) for i in range(ends)]),
                cells,
                lax.ppermute(head, axis, [((i + 1) % count, i) for i in range(ends)]),
            ],
            axis=dim,
        )
    return cells


def from_root(block, axis, source):
    block = jnp.where(lax.axis_index(axis) == source, block, jnp.zeros_like(block))
    return lax.psum(block, axis)


def lag_table(first_bin):
    bin_number = first_bin + jnp.arange(BAND_BINS, dtype=jnp.int32)
    lag_number = jnp.arange(LAGS, dtype=jnp.int32) - LAGS // 2
    phase_steps = jnp.remainder(lag_number[:, None] * bin_number[None, :], 2 * BAND_BINS)
    phases = phase_steps.astype(jnp.float32) * (math.pi / BAND_BINS)
    normalizer = 1.0 / math.sqrt(SEGS * BAND_BINS)
    weights = jnp.stack([jnp.cos(phases), -jnp.sin(phases)], axis=2) * normalizer
    return weights.astype(jnp.bfloat16).reshape(LAGS, 2 * BAND_BINS)


def cross_terms(sources, receivers):
    src_real = sources[:, 0]
    src_imag = sources[:, 1]
    left_stack = jnp.stack(
        [jnp.concatenate([src_real, src_imag], 0), jnp.concatenate([src_imag, -src_real], 0)], 0
    )
    right_stack = jnp.concatenate([receivers[:, 0], receivers[:, 1]], 0)
    cross_spectra = jnp.einsum(
        "ctfs,tfn->fcsn", left_stack, right_stack, preferred_element_type=jnp.float32
    )
    return cross_spectra.astype(jnp.bfloat16)


def local(spectra, plan, pair_mask):
    seg_local = spectra.shape[0]
    band_bins = spectra.shape[2]
    sta_local = spectra.shape[3]
    band_position = lax.axis_index("band")
    sta_position = lax.axis_index("sta")
    seg_position = lax.axis_index("seg")
    total_bins = band_bins * lax.axis_size("band")
    half_sources = SRC // lax.axis_size("seg")
    amplitude = jnp.sqrt(spectra[:, 0] ** 2 + spectra[:, 1] ** 2)
    extended = padded(amplitude, (("band", 1),), HALF)
    block_width = 2 * HALF
    block_count = band_bins // block_width
    lower_part = extended[:, : block_count * block_width].reshape(
        seg_local, block_count, block_width, sta_local
    )
    upper_part = extended[:, block_width:].reshape(seg_local, block_count, block_width, sta_local)
    windows = jnp.concatenate([lower_part, upper_part], axis=2)
    offsets = jnp.arange(2 * block_width, dtype=jnp.int32)[:, None]
    targets = jnp.arange(block_width, dtype=jnp.int32)[None, :]
    band_matrix = ((offsets >= targets) & (offsets <= targets + 2 * HALF)).astype(jnp.float32)
    window_sums = jnp.einsum("tbgn,gf->tbfn", windows, band_matrix, precision=lax.Precision.HIGHEST)
    window_sums = window_sums.reshape(seg_local, band_bins, sta_local)
    bin_number = band_position * band_bins + jnp.arange(band_bins, dtype=jnp.int32)
    in_range = (
        jnp.minimum(bin_number + HALF, total_bins - 1) - jnp.maximum(bin_number - HALF, 0) + 1
    ).astype(jnp.float32)
    smooth = window_sums / in_range[None, :, None]
    white = (spectra / (smooth[:, None] + EPSILON)).astype(jnp.bfloat16)
    receivers = lax.all_gather(white, "seg", axis=0, tiled=True)
    own_half = lax.all_to_all(white, "seg", split_axis=3, concat_axis=0, tiled=True)
    candidates = lax.all_gather(own_half, "sta", axis=0, tiled=False)
    blk_dev = sta_local // SRC
    lag_weights = lag_table(band_position * band_bins).reshape(LAGS, band_bins, 2)
    receiver_ids = sta_position * sta_local + jnp.arange(sta_local, dtype=jnp.int32)
    block_columns = jnp.arange(pair_mask.shape[1], dtype=jnp.int32)
    block_onehot = ((receiver_ids // SRC)[:, None] == block_columns[None, :]).astype(jnp.float32)
    results = []
    for step_number in range(STEPS):
        block_number = plan[step_number]
        owner_position = block_number // blk_dev
        held = lax.dynamic_index_in_dim(candidates, owner_position, 0, keepdims=False)
        sources = lax.dynamic_slice_in_dim(
            held, (block_number % blk_dev) * half_sources, half_sources, 3
        )
        cross_spectra = cross_terms(sources, receivers)
        correlated = lax.dot_general(
            lag_weights,
            cross_spectra,
            (((1, 2), (0, 1)), ((), ())),
            preferred_element_type=jnp.float32,
        )
        mask_row = pair_mask[block_number].astype(jnp.float32)
        allowed = jnp.sum(block_onehot * mask_row[None, :], axis=1)
        source_ids = (
            block_number * SRC
            + seg_position * half_sources
            + jnp.arange(half_sources, dtype=jnp.int32)
        )
        keep_pairs = (source_ids[:, None] != receiver_ids[None, :]).astype(jnp.float32) * allowed[
            None, :
        ]
        results.append((correlated * keep_pairs[None]).astype(jnp.bfloat16))
    return jnp.stack(results, 0)


def solution(mesh):
    return jax.shard_map(
        local,
        mesh=mesh,
        in_specs=(P("seg", None, "band", ("groups", "sta")), P("groups"), P("groups", None)),
        out_specs=P(None, "band", "seg", ("groups", "sta")),
        check_vma=False,
    )
```

```python
import math

import jax
import jax.numpy as jnp
from jax import lax
from jax.sharding import PartitionSpec as P

SEGS = 8
STEPS = 2
SRC = 128
BLK_DEV = 1
BAND_BINS = 256
HALF = 64
LAGS = 128


EPSILON = 1e-06


def padded(cells, sides, width):
    for axis, dim in sides:
        count = lax.axis_size(axis)
        ends = count - 1
        head = lax.slice_in_dim(cells, 0, width, axis=dim)
        tail = lax.slice_in_dim(cells, cells.shape[dim] - width, cells.shape[dim], axis=dim)
        cells = jnp.concatenate(
            [
                lax.ppermute(tail, axis, [(i, (i + 1) % count) for i in range(ends)]),
                cells,
                lax.ppermute(head, axis, [((i + 1) % count, i) for i in range(ends)]),
            ],
            axis=dim,
        )
    return cells


def from_root(block, axis, source):
    block = jnp.where(lax.axis_index(axis) == source, block, jnp.zeros_like(block))
    return lax.psum(block, axis)


def lag_table(first_bin):
    bin_number = first_bin + jnp.arange(BAND_BINS, dtype=jnp.int32)
    lag_number = jnp.arange(LAGS, dtype=jnp.int32) - LAGS // 2
    phase_steps = jnp.remainder(lag_number[:, None] * bin_number[None, :], 2 * BAND_BINS)
    phases = phase_steps.astype(jnp.float32) * (math.pi / BAND_BINS)
    normalizer = 1.0 / math.sqrt(SEGS * BAND_BINS)
    weights = jnp.stack([jnp.cos(phases), -jnp.sin(phases)], axis=2) * normalizer
    return weights.astype(jnp.bfloat16).reshape(LAGS, 2 * BAND_BINS)


def cross_terms(sources, receivers):
    src_real = sources[:, 0]
    src_imag = sources[:, 1]
    left_stack = jnp.stack(
        [jnp.concatenate([src_real, src_imag], 0), jnp.concatenate([src_imag, -src_real], 0)], 0
    )
    right_stack = jnp.concatenate([receivers[:, 0], receivers[:, 1]], 0)
    cross_spectra = jnp.einsum(
        "ctfs,tfn->fcsn", left_stack, right_stack, preferred_element_type=jnp.float32
    )
    return cross_spectra.astype(jnp.bfloat16)


def local(spectra, plan, pair_mask):
    seg_local = spectra.shape[0]
    band_bins = spectra.shape[2]
    sta_local = spectra.shape[3]
    band_position = lax.axis_index("band")
    sta_position = lax.axis_index("sta")
    seg_position = lax.axis_index("seg")
    total_bins = band_bins * lax.axis_size("band")
    half_sources = SRC // lax.axis_size("seg")
    amplitude = jnp.sqrt(spectra[:, 0] ** 2 + spectra[:, 1] ** 2)
    extended = padded(amplitude, (("band", 1),), HALF)
    block_width = 2 * HALF
    block_count = band_bins // block_width
    lower_part = extended[:, : block_count * block_width].reshape(
        seg_local, block_count, block_width, sta_local
    )
    upper_part = extended[:, block_width:].reshape(seg_local, block_count, block_width, sta_local)
    windows = jnp.concatenate([lower_part, upper_part], axis=2)
    offsets = jnp.arange(2 * block_width, dtype=jnp.int32)[:, None]
    targets = jnp.arange(block_width, dtype=jnp.int32)[None, :]
    band_matrix = ((offsets >= targets) & (offsets <= targets + 2 * HALF)).astype(jnp.float32)
    window_sums = jnp.einsum("tbgn,gf->tbfn", windows, band_matrix, precision=lax.Precision.HIGHEST)
    window_sums = window_sums.reshape(seg_local, band_bins, sta_local)
    bin_number = band_position * band_bins + jnp.arange(band_bins, dtype=jnp.int32)
    in_range = (
        jnp.minimum(bin_number + HALF, total_bins - 1) - jnp.maximum(bin_number - HALF, 0) + 1
    ).astype(jnp.float32)
    smooth = window_sums / in_range[None, :, None]
    white = (spectra / (smooth[:, None] + EPSILON)).astype(jnp.bfloat16)
    seg_count = lax.axis_size("seg")
    sta_count = lax.axis_size("sta")
    receivers = lax.all_gather(white, "seg", axis=0, tiled=True) if seg_count > 2 else None
    if receivers is None:
        partner = lax.ppermute(white, "seg", [(0, 1), (1, 0)])
        receivers = jnp.where(
            seg_position == 0,
            jnp.concatenate([white, partner], 0),
            jnp.concatenate([partner, white], 0),
        )
    own_half = lax.dynamic_slice_in_dim(receivers, seg_position * half_sources, half_sources, 3)
    shifted = [own_half]
    for shift in range(1, sta_count):
        shifted.append(
            lax.ppermute(own_half, "sta", [(i, (i + shift) % sta_count) for i in range(sta_count)])
        )
    candidates = jnp.stack(shifted, 0)
    blk_dev = sta_local // SRC
    lag_weights = lag_table(band_position * band_bins).reshape(LAGS, band_bins, 2)
    receiver_ids = sta_position * sta_local + jnp.arange(sta_local, dtype=jnp.int32)
    block_columns = jnp.arange(pair_mask.shape[1], dtype=jnp.int32)
    block_onehot = ((receiver_ids // SRC)[:, None] == block_columns[None, :]).astype(jnp.float32)
    results = []
    for step_number in range(STEPS):
        block_number = plan[step_number]
        owner_position = block_number // blk_dev
        distance = (sta_position - owner_position) % sta_count
        held = lax.dynamic_index_in_dim(candidates, distance, 0, keepdims=False)
        sources = lax.dynamic_slice_in_dim(
            held, (block_number % blk_dev) * half_sources, half_sources, 3
        )
        cross_spectra = cross_terms(sources, receivers)
        correlated = lax.dot_general(
            lag_weights,
            cross_spectra,
            (((1, 2), (0, 1)), ((), ())),
            preferred_element_type=jnp.float32,
        )
        mask_row = pair_mask[block_number].astype(jnp.float32)
        allowed = jnp.sum(block_onehot * mask_row[None, :], axis=1)
        source_ids = (
            block_number * SRC
            + seg_position * half_sources
            + jnp.arange(half_sources, dtype=jnp.int32)
        )
        keep_pairs = (source_ids[:, None] != receiver_ids[None, :]).astype(jnp.float32) * allowed[
            None, :
        ]
        results.append((correlated * keep_pairs[None]).astype(jnp.bfloat16))
    return jnp.stack(results, 0)


def solution(mesh):
    return jax.shard_map(
        local,
        mesh=mesh,
        in_specs=(P("seg", None, "band", ("groups", "sta")), P("groups"), P("groups", None)),
        out_specs=P(None, "band", "seg", ("groups", "sta")),
        check_vma=False,
    )
```

```python
import math

import jax
import jax.numpy as jnp
from jax import lax
from jax.sharding import PartitionSpec as P

SEGS = 8
STEPS = 2
SRC = 128
BLK_DEV = 1
BAND_BINS = 256
HALF = 64
LAGS = 128
CHUNKS = 2


EPSILON = 1e-06


def padded(cells, sides, width):
    for axis, dim in sides:
        count = lax.axis_size(axis)
        ends = count - 1
        head = lax.slice_in_dim(cells, 0, width, axis=dim)
        tail = lax.slice_in_dim(cells, cells.shape[dim] - width, cells.shape[dim], axis=dim)
        cells = jnp.concatenate(
            [
                lax.ppermute(tail, axis, [(i, (i + 1) % count) for i in range(ends)]),
                cells,
                lax.ppermute(head, axis, [((i + 1) % count, i) for i in range(ends)]),
            ],
            axis=dim,
        )
    return cells


def from_root(block, axis, source):
    block = jnp.where(lax.axis_index(axis) == source, block, jnp.zeros_like(block))
    return lax.psum(block, axis)


def lag_table(first_bin):
    bin_number = first_bin + jnp.arange(BAND_BINS, dtype=jnp.int32)
    lag_number = jnp.arange(LAGS, dtype=jnp.int32) - LAGS // 2
    phase_steps = jnp.remainder(lag_number[:, None] * bin_number[None, :], 2 * BAND_BINS)
    phases = phase_steps.astype(jnp.float32) * (math.pi / BAND_BINS)
    normalizer = 1.0 / math.sqrt(SEGS * BAND_BINS)
    weights = jnp.stack([jnp.cos(phases), -jnp.sin(phases)], axis=2) * normalizer
    return weights.astype(jnp.bfloat16).reshape(LAGS, 2 * BAND_BINS)


def cross_terms(sources, receivers):
    src_real = sources[:, 0]
    src_imag = sources[:, 1]
    left_stack = jnp.stack(
        [jnp.concatenate([src_real, src_imag], 0), jnp.concatenate([src_imag, -src_real], 0)], 0
    )
    right_stack = jnp.concatenate([receivers[:, 0], receivers[:, 1]], 0)
    cross_spectra = jnp.einsum(
        "ctfs,tfn->fcsn", left_stack, right_stack, preferred_element_type=jnp.float32
    )
    return cross_spectra.astype(jnp.bfloat16)


def local(spectra, plan, pair_mask):
    seg_local = spectra.shape[0]
    band_bins = spectra.shape[2]
    sta_local = spectra.shape[3]
    band_position = lax.axis_index("band")
    sta_position = lax.axis_index("sta")
    seg_position = lax.axis_index("seg")
    total_bins = band_bins * lax.axis_size("band")
    half_sources = SRC // lax.axis_size("seg")
    amplitude = jnp.sqrt(spectra[:, 0] ** 2 + spectra[:, 1] ** 2)
    extended = padded(amplitude, (("band", 1),), HALF)
    block_width = 2 * HALF
    block_count = band_bins // block_width
    lower_part = extended[:, : block_count * block_width].reshape(
        seg_local, block_count, block_width, sta_local
    )
    upper_part = extended[:, block_width:].reshape(seg_local, block_count, block_width, sta_local)
    windows = jnp.concatenate([lower_part, upper_part], axis=2)
    offsets = jnp.arange(2 * block_width, dtype=jnp.int32)[:, None]
    targets = jnp.arange(block_width, dtype=jnp.int32)[None, :]
    band_matrix = ((offsets >= targets) & (offsets <= targets + 2 * HALF)).astype(jnp.float32)
    window_sums = jnp.einsum("tbgn,gf->tbfn", windows, band_matrix, precision=lax.Precision.HIGHEST)
    window_sums = window_sums.reshape(seg_local, band_bins, sta_local)
    bin_number = band_position * band_bins + jnp.arange(band_bins, dtype=jnp.int32)
    in_range = (
        jnp.minimum(bin_number + HALF, total_bins - 1) - jnp.maximum(bin_number - HALF, 0) + 1
    ).astype(jnp.float32)
    smooth = window_sums / in_range[None, :, None]
    white = (spectra / (smooth[:, None] + EPSILON)).astype(jnp.bfloat16)
    seg_count = lax.axis_size("seg")
    sta_count = lax.axis_size("sta")
    receivers = lax.all_gather(white, "seg", axis=0, tiled=True) if seg_count > 2 else None
    if receivers is None:
        partner = lax.ppermute(white, "seg", [(0, 1), (1, 0)])
        receivers = jnp.where(
            seg_position == 0,
            jnp.concatenate([white, partner], 0),
            jnp.concatenate([partner, white], 0),
        )
    own_half = lax.dynamic_slice_in_dim(receivers, seg_position * half_sources, half_sources, 3)
    blk_dev = sta_local // SRC
    lag_weights = lag_table(band_position * band_bins).reshape(LAGS, band_bins, 2)
    receiver_ids = sta_position * sta_local + jnp.arange(sta_local, dtype=jnp.int32)
    block_columns = jnp.arange(pair_mask.shape[1], dtype=jnp.int32)
    block_onehot = ((receiver_ids // SRC)[:, None] == block_columns[None, :]).astype(jnp.float32)
    chunks = CHUNKS if half_sources % CHUNKS == 0 else 1
    width = half_sources // chunks
    pieces = [[] for _ in range(STEPS)]
    arrived = None
    for chunk in range(chunks):
        piece = lax.slice_in_dim(own_half, chunk * width, (chunk + 1) * width, axis=3)
        if arrived is not None:
            piece, _ = lax.optimization_barrier((piece, arrived))
        shifted = [piece]
        for shift in range(1, sta_count):
            shifted.append(
                lax.ppermute(piece, "sta", [(i, (i + shift) % sta_count) for i in range(sta_count)])
            )
        arrived = shifted[1:]
        candidates = jnp.stack(shifted, 0)
        for step_number in range(STEPS):
            block_number = plan[step_number]
            owner_position = block_number // blk_dev
            distance = (sta_position - owner_position) % sta_count
            held = lax.dynamic_index_in_dim(candidates, distance, 0, keepdims=False)
            sources = lax.dynamic_slice_in_dim(
                held, (block_number % blk_dev) * width, width, 3
            )
            cross_spectra = cross_terms(sources, receivers)
            pieces[step_number].append(
                lax.dot_general(
                    lag_weights,
                    cross_spectra,
                    (((1, 2), (0, 1)), ((), ())),
                    preferred_element_type=jnp.float32,
                )
            )
    results = []
    for step_number in range(STEPS):
        block_number = plan[step_number]
        correlated = jnp.concatenate(pieces[step_number], 1)
        mask_row = pair_mask[block_number].astype(jnp.float32)
        allowed = jnp.sum(block_onehot * mask_row[None, :], axis=1)
        source_ids = (
            block_number * SRC
            + seg_position * half_sources
            + jnp.arange(half_sources, dtype=jnp.int32)
        )
        keep_pairs = (source_ids[:, None] != receiver_ids[None, :]).astype(jnp.float32) * allowed[
            None, :
        ]
        results.append((correlated * keep_pairs[None]).astype(jnp.bfloat16))
    return jnp.stack(results, 0)


def solution(mesh):
    return jax.shard_map(
        local,
        mesh=mesh,
        in_specs=(P("seg", None, "band", ("groups", "sta")), P("groups"), P("groups", None)),
        out_specs=P(None, "band", "seg", ("groups", "sta")),
        check_vma=False,
    )
```

```python
import math

import jax
import jax.numpy as jnp
from jax import lax
from jax.sharding import PartitionSpec as P

SEGS = 8
STEPS = 2
SRC = 128
BLK_DEV = 1
BAND_BINS = 256
HALF = 64
LAGS = 128


EPSILON = 1e-06


def padded(cells, sides, width):
    for axis, dim in sides:
        count = lax.axis_size(axis)
        ends = count - 1
        head = lax.slice_in_dim(cells, 0, width, axis=dim)
        tail = lax.slice_in_dim(cells, cells.shape[dim] - width, cells.shape[dim], axis=dim)
        cells = jnp.concatenate(
            [
                lax.ppermute(tail, axis, [(i, (i + 1) % count) for i in range(ends)]),
                cells,
                lax.ppermute(head, axis, [((i + 1) % count, i) for i in range(ends)]),
            ],
            axis=dim,
        )
    return cells


def from_root(block, axis, source):
    block = jnp.where(lax.axis_index(axis) == source, block, jnp.zeros_like(block))
    return lax.psum(block, axis)


def lag_table(first_bin):
    bin_number = first_bin + jnp.arange(BAND_BINS, dtype=jnp.int32)
    lag_number = jnp.arange(LAGS, dtype=jnp.int32) - LAGS // 2
    phase_steps = jnp.remainder(lag_number[:, None] * bin_number[None, :], 2 * BAND_BINS)
    phases = phase_steps.astype(jnp.float32) * (math.pi / BAND_BINS)
    normalizer = 1.0 / math.sqrt(SEGS * BAND_BINS)
    weights = jnp.stack([jnp.cos(phases), -jnp.sin(phases)], axis=2) * normalizer
    return weights.astype(jnp.bfloat16).reshape(LAGS, 2 * BAND_BINS)


def cross_terms(sources, receivers):
    src_real = sources[:, 0]
    src_imag = sources[:, 1]
    left_stack = jnp.stack(
        [jnp.concatenate([src_real, src_imag], 0), jnp.concatenate([src_imag, -src_real], 0)], 0
    )
    right_stack = jnp.concatenate([receivers[:, 0], receivers[:, 1]], 0)
    cross_spectra = jnp.einsum(
        "ctfs,tfn->fcsn", left_stack, right_stack, preferred_element_type=jnp.float32
    )
    return cross_spectra.astype(jnp.bfloat16)


def local(spectra, plan, pair_mask):
    seg_local = spectra.shape[0]
    band_bins = spectra.shape[2]
    sta_local = spectra.shape[3]
    band_position = lax.axis_index("band")
    sta_position = lax.axis_index("sta")
    seg_position = lax.axis_index("seg")
    total_bins = band_bins * lax.axis_size("band")
    half_sources = SRC // lax.axis_size("seg")
    amplitude = jnp.sqrt(spectra[:, 0] ** 2 + spectra[:, 1] ** 2)
    extended = padded(amplitude, (("band", 1),), HALF)
    block_width = 2 * HALF
    block_count = band_bins // block_width
    lower_part = extended[:, : block_count * block_width].reshape(
        seg_local, block_count, block_width, sta_local
    )
    upper_part = extended[:, block_width:].reshape(seg_local, block_count, block_width, sta_local)
    windows = jnp.concatenate([lower_part, upper_part], axis=2)
    offsets = jnp.arange(2 * block_width, dtype=jnp.int32)[:, None]
    targets = jnp.arange(block_width, dtype=jnp.int32)[None, :]
    band_matrix = ((offsets >= targets) & (offsets <= targets + 2 * HALF)).astype(jnp.float32)
    window_sums = jnp.einsum("tbgn,gf->tbfn", windows, band_matrix, precision=lax.Precision.HIGHEST)
    window_sums = window_sums.reshape(seg_local, band_bins, sta_local)
    bin_number = band_position * band_bins + jnp.arange(band_bins, dtype=jnp.int32)
    in_range = (
        jnp.minimum(bin_number + HALF, total_bins - 1) - jnp.maximum(bin_number - HALF, 0) + 1
    ).astype(jnp.float32)
    smooth = window_sums / in_range[None, :, None]
    white = (spectra / (smooth[:, None] + EPSILON)).astype(jnp.bfloat16)
    seg_count = lax.axis_size("seg")
    sta_count = lax.axis_size("sta")
    receivers = lax.all_gather(white, "seg", axis=0, tiled=True) if seg_count > 2 else None
    if receivers is None:
        partner = lax.ppermute(white, "seg", [(0, 1), (1, 0)])
        receivers = jnp.where(
            seg_position == 0,
            jnp.concatenate([white, partner], 0),
            jnp.concatenate([partner, white], 0),
        )
    own_half = lax.dynamic_slice_in_dim(receivers, seg_position * half_sources, half_sources, 3)
    rightward = [(i, i + 1) for i in range(sta_count - 1)]
    leftward = [(i + 1, i) for i in range(sta_count - 1)]
    from_left = [own_half]
    from_right = [own_half]
    for _ in range(1, sta_count):
        from_left.append(lax.ppermute(from_left[-1], "sta", rightward))
        from_right.append(lax.ppermute(from_right[-1], "sta", leftward))
    candidates = jnp.stack(from_left + from_right[1:], 0)
    blk_dev = sta_local // SRC
    lag_weights = lag_table(band_position * band_bins).reshape(LAGS, band_bins, 2)
    receiver_ids = sta_position * sta_local + jnp.arange(sta_local, dtype=jnp.int32)
    block_columns = jnp.arange(pair_mask.shape[1], dtype=jnp.int32)
    block_onehot = ((receiver_ids // SRC)[:, None] == block_columns[None, :]).astype(jnp.float32)
    results = []
    for step_number in range(STEPS):
        block_number = plan[step_number]
        owner_position = block_number // blk_dev
        distance = jnp.where(
            owner_position <= sta_position,
            sta_position - owner_position,
            sta_count - 1 + owner_position - sta_position,
        )
        held = lax.dynamic_index_in_dim(candidates, distance, 0, keepdims=False)
        sources = lax.dynamic_slice_in_dim(
            held, (block_number % blk_dev) * half_sources, half_sources, 3
        )
        cross_spectra = cross_terms(sources, receivers)
        correlated = lax.dot_general(
            lag_weights,
            cross_spectra,
            (((1, 2), (0, 1)), ((), ())),
            preferred_element_type=jnp.float32,
        )
        mask_row = pair_mask[block_number].astype(jnp.float32)
        allowed = jnp.sum(block_onehot * mask_row[None, :], axis=1)
        source_ids = (
            block_number * SRC
            + seg_position * half_sources
            + jnp.arange(half_sources, dtype=jnp.int32)
        )
        keep_pairs = (source_ids[:, None] != receiver_ids[None, :]).astype(jnp.float32) * allowed[
            None, :
        ]
        results.append((correlated * keep_pairs[None]).astype(jnp.bfloat16))
    return jnp.stack(results, 0)


def solution(mesh):
    return jax.shard_map(
        local,
        mesh=mesh,
        in_specs=(P("seg", None, "band", ("groups", "sta")), P("groups"), P("groups", None)),
        out_specs=P(None, "band", "seg", ("groups", "sta")),
        check_vma=False,
    )
```

```python
import math

import jax
import jax.numpy as jnp
from jax import lax
from jax.sharding import PartitionSpec as P

SEGS = 8
STEPS = 2
SRC = 128
BLK_DEV = 1
BAND_BINS = 256
HALF = 64
LAGS = 128


EPSILON = 1e-06


def padded(cells, sides, width):
    for axis, dim in sides:
        count = lax.axis_size(axis)
        ends = count - 1
        head = lax.slice_in_dim(cells, 0, width, axis=dim)
        tail = lax.slice_in_dim(cells, cells.shape[dim] - width, cells.shape[dim], axis=dim)
        if count == 2:
            first = lax.axis_index(axis) == 0
            swapped = lax.ppermute(jnp.where(first, tail, head), axis, [(0, 1), (1, 0)])
            zeros = jnp.zeros_like(swapped)
            lower = jnp.where(first, zeros, swapped)
            upper = jnp.where(first, swapped, zeros)
        else:
            lower = lax.ppermute(tail, axis, [(i, (i + 1) % count) for i in range(ends)])
            upper = lax.ppermute(head, axis, [((i + 1) % count, i) for i in range(ends)])
        cells = jnp.concatenate([lower, cells, upper], axis=dim)
    return cells


def from_root(block, axis, source):
    block = jnp.where(lax.axis_index(axis) == source, block, jnp.zeros_like(block))
    return lax.psum(block, axis)


def lag_table(first_bin):
    bin_number = first_bin + jnp.arange(BAND_BINS, dtype=jnp.int32)
    lag_number = jnp.arange(LAGS, dtype=jnp.int32) - LAGS // 2
    phase_steps = jnp.remainder(lag_number[:, None] * bin_number[None, :], 2 * BAND_BINS)
    phases = phase_steps.astype(jnp.float32) * (math.pi / BAND_BINS)
    normalizer = 1.0 / math.sqrt(SEGS * BAND_BINS)
    weights = jnp.stack([jnp.cos(phases), -jnp.sin(phases)], axis=2) * normalizer
    return weights.astype(jnp.bfloat16).reshape(LAGS, 2 * BAND_BINS)


def cross_terms(sources, receivers):
    src_real = sources[:, 0]
    src_imag = sources[:, 1]
    left_stack = jnp.stack(
        [jnp.concatenate([src_real, src_imag], 0), jnp.concatenate([src_imag, -src_real], 0)], 0
    )
    right_stack = jnp.concatenate([receivers[:, 0], receivers[:, 1]], 0)
    cross_spectra = jnp.einsum(
        "ctfs,tfn->fcsn", left_stack, right_stack, preferred_element_type=jnp.float32
    )
    return cross_spectra.astype(jnp.bfloat16)


def local(spectra, plan, pair_mask):
    seg_local = spectra.shape[0]
    band_bins = spectra.shape[2]
    sta_local = spectra.shape[3]
    band_position = lax.axis_index("band")
    sta_position = lax.axis_index("sta")
    seg_position = lax.axis_index("seg")
    total_bins = band_bins * lax.axis_size("band")
    half_sources = SRC // lax.axis_size("seg")
    amplitude = jnp.sqrt(spectra[:, 0] ** 2 + spectra[:, 1] ** 2)
    extended = padded(amplitude, (("band", 1),), HALF)
    block_width = 2 * HALF
    block_count = band_bins // block_width
    lower_part = extended[:, : block_count * block_width].reshape(
        seg_local, block_count, block_width, sta_local
    )
    upper_part = extended[:, block_width:].reshape(seg_local, block_count, block_width, sta_local)
    windows = jnp.concatenate([lower_part, upper_part], axis=2)
    offsets = jnp.arange(2 * block_width, dtype=jnp.int32)[:, None]
    targets = jnp.arange(block_width, dtype=jnp.int32)[None, :]
    band_matrix = ((offsets >= targets) & (offsets <= targets + 2 * HALF)).astype(jnp.float32)
    window_sums = jnp.einsum("tbgn,gf->tbfn", windows, band_matrix, precision=lax.Precision.HIGHEST)
    window_sums = window_sums.reshape(seg_local, band_bins, sta_local)
    bin_number = band_position * band_bins + jnp.arange(band_bins, dtype=jnp.int32)
    in_range = (
        jnp.minimum(bin_number + HALF, total_bins - 1) - jnp.maximum(bin_number - HALF, 0) + 1
    ).astype(jnp.float32)
    smooth = window_sums / in_range[None, :, None]
    white = (spectra / (smooth[:, None] + EPSILON)).astype(jnp.bfloat16)
    seg_count = lax.axis_size("seg")
    sta_count = lax.axis_size("sta")
    partner = lax.ppermute(white, "seg", [(h, (h + 1) % seg_count) for h in range(seg_count)])
    receivers = jnp.concatenate([white, partner], 0)
    halves = [
        lax.dynamic_slice_in_dim(
            white, ((seg_position + offset) % seg_count) * half_sources, half_sources, 3
        )
        for offset in range(seg_count)
    ]
    own_half = lax.dynamic_slice_in_dim(receivers, seg_position * half_sources, half_sources, 3)
    shifted = [own_half]
    for shift in range(1, sta_count):
        pieces = []
        for offset in range(seg_count):
            pairs = [
                (i * seg_count + h, ((i + shift) % sta_count) * seg_count + (h + offset) % seg_count)
                for i in range(sta_count)
                for h in range(seg_count)
            ]
            pieces.append(lax.ppermute(halves[offset], ("sta", "seg"), pairs))
        shifted.append(jnp.concatenate(pieces, 0))
    candidates = jnp.stack(shifted, 0)
    blk_dev = sta_local // SRC
    lag_weights = lag_table(band_position * band_bins).reshape(LAGS, band_bins, 2)
    receiver_ids = sta_position * sta_local + jnp.arange(sta_local, dtype=jnp.int32)
    block_columns = jnp.arange(pair_mask.shape[1], dtype=jnp.int32)
    block_onehot = ((receiver_ids // SRC)[:, None] == block_columns[None, :]).astype(jnp.float32)
    results = []
    for step_number in range(STEPS):
        block_number = plan[step_number]
        owner_position = block_number // blk_dev
        distance = (sta_position - owner_position) % sta_count
        held = lax.dynamic_index_in_dim(candidates, distance, 0, keepdims=False)
        sources = lax.dynamic_slice_in_dim(
            held, (block_number % blk_dev) * half_sources, half_sources, 3
        )
        cross_spectra = cross_terms(sources, receivers)
        correlated = lax.dot_general(
            lag_weights,
            cross_spectra,
            (((1, 2), (0, 1)), ((), ())),
            preferred_element_type=jnp.float32,
        )
        mask_row = pair_mask[block_number].astype(jnp.float32)
        allowed = jnp.sum(block_onehot * mask_row[None, :], axis=1)
        source_ids = (
            block_number * SRC
            + seg_position * half_sources
            + jnp.arange(half_sources, dtype=jnp.int32)
        )
        keep_pairs = (source_ids[:, None] != receiver_ids[None, :]).astype(jnp.float32) * allowed[
            None, :
        ]
        results.append((correlated * keep_pairs[None]).astype(jnp.bfloat16))
    return jnp.stack(results, 0)


def solution(mesh):
    return jax.shard_map(
        local,
        mesh=mesh,
        in_specs=(P("seg", None, "band", ("groups", "sta")), P("groups"), P("groups", None)),
        out_specs=P(None, "band", "seg", ("groups", "sta")),
        check_vma=False,
    )
```

```python
import math

import jax
import jax.numpy as jnp
from jax import lax
from jax.sharding import PartitionSpec as P

SEGS = 8
STEPS = 2
SRC = 128
BLK_DEV = 1
BAND_BINS = 256
HALF = 64
LAGS = 128


EPSILON = 1e-06


def padded(cells, sides, width):
    for axis, dim in sides:
        count = lax.axis_size(axis)
        ends = count - 1
        head = lax.slice_in_dim(cells, 0, width, axis=dim)
        tail = lax.slice_in_dim(cells, cells.shape[dim] - width, cells.shape[dim], axis=dim)
        if count == 2:
            first = lax.axis_index(axis) == 0
            swapped = lax.ppermute(jnp.where(first, tail, head), axis, [(0, 1), (1, 0)])
            zeros = jnp.zeros_like(swapped)
            lower = jnp.where(first, zeros, swapped)
            upper = jnp.where(first, swapped, zeros)
        else:
            lower = lax.ppermute(tail, axis, [(i, (i + 1) % count) for i in range(ends)])
            upper = lax.ppermute(head, axis, [((i + 1) % count, i) for i in range(ends)])
        cells = jnp.concatenate([lower, cells, upper], axis=dim)
    return cells


def from_root(block, axis, source):
    block = jnp.where(lax.axis_index(axis) == source, block, jnp.zeros_like(block))
    return lax.psum(block, axis)


def lag_table(first_bin):
    bin_number = first_bin + jnp.arange(BAND_BINS, dtype=jnp.int32)
    lag_number = jnp.arange(LAGS, dtype=jnp.int32) - LAGS // 2
    phase_steps = jnp.remainder(lag_number[:, None] * bin_number[None, :], 2 * BAND_BINS)
    phases = phase_steps.astype(jnp.float32) * (math.pi / BAND_BINS)
    normalizer = 1.0 / math.sqrt(SEGS * BAND_BINS)
    weights = jnp.stack([jnp.cos(phases), -jnp.sin(phases)], axis=2) * normalizer
    return weights.astype(jnp.bfloat16).reshape(LAGS, 2 * BAND_BINS)


def cross_terms(sources, receivers):
    src_real = sources[:, 0]
    src_imag = sources[:, 1]
    left_stack = jnp.stack(
        [jnp.concatenate([src_real, src_imag], 0), jnp.concatenate([src_imag, -src_real], 0)], 0
    )
    right_stack = jnp.concatenate([receivers[:, 0], receivers[:, 1]], 0)
    cross_spectra = jnp.einsum(
        "ctfs,tfn->fcsn", left_stack, right_stack, preferred_element_type=jnp.float32
    )
    return cross_spectra.astype(jnp.bfloat16)


def local(spectra, plan, pair_mask):
    seg_local = spectra.shape[0]
    band_bins = spectra.shape[2]
    sta_local = spectra.shape[3]
    band_position = lax.axis_index("band")
    sta_position = lax.axis_index("sta")
    seg_position = lax.axis_index("seg")
    total_bins = band_bins * lax.axis_size("band")
    half_sources = SRC // lax.axis_size("seg")
    amplitude = jnp.sqrt(spectra[:, 0] ** 2 + spectra[:, 1] ** 2)
    extended = padded(amplitude, (("band", 1),), HALF)
    block_width = 2 * HALF
    block_count = band_bins // block_width
    lower_part = extended[:, : block_count * block_width].reshape(
        seg_local, block_count, block_width, sta_local
    )
    upper_part = extended[:, block_width:].reshape(seg_local, block_count, block_width, sta_local)
    windows = jnp.concatenate([lower_part, upper_part], axis=2)
    offsets = jnp.arange(2 * block_width, dtype=jnp.int32)[:, None]
    targets = jnp.arange(block_width, dtype=jnp.int32)[None, :]
    band_matrix = ((offsets >= targets) & (offsets <= targets + 2 * HALF)).astype(jnp.float32)
    window_sums = jnp.einsum("tbgn,gf->tbfn", windows, band_matrix, precision=lax.Precision.HIGHEST)
    window_sums = window_sums.reshape(seg_local, band_bins, sta_local)
    bin_number = band_position * band_bins + jnp.arange(band_bins, dtype=jnp.int32)
    in_range = (
        jnp.minimum(bin_number + HALF, total_bins - 1) - jnp.maximum(bin_number - HALF, 0) + 1
    ).astype(jnp.float32)
    smooth = window_sums / in_range[None, :, None]
    white = (spectra / (smooth[:, None] + EPSILON)).astype(jnp.bfloat16)
    seg_count = lax.axis_size("seg")
    sta_count = lax.axis_size("sta")
    receivers = lax.all_gather(white, "seg", axis=0, tiled=True) if seg_count > 2 else None
    if receivers is None:
        partner = lax.ppermute(white, "seg", [(0, 1), (1, 0)])
        receivers = jnp.where(
            seg_position == 0,
            jnp.concatenate([white, partner], 0),
            jnp.concatenate([partner, white], 0),
        )
    own_half = lax.dynamic_slice_in_dim(receivers, seg_position * half_sources, half_sources, 3)
    shifted = [own_half]
    for shift in range(1, sta_count):
        shifted.append(
            lax.ppermute(own_half, "sta", [(i, (i + shift) % sta_count) for i in range(sta_count)])
        )
    candidates = jnp.stack(shifted, 0)
    blk_dev = sta_local // SRC
    lag_weights = lag_table(band_position * band_bins).reshape(LAGS, band_bins, 2)
    receiver_ids = sta_position * sta_local + jnp.arange(sta_local, dtype=jnp.int32)
    block_columns = jnp.arange(pair_mask.shape[1], dtype=jnp.int32)
    block_onehot = ((receiver_ids // SRC)[:, None] == block_columns[None, :]).astype(jnp.float32)
    results = []
    for step_number in range(STEPS):
        block_number = plan[step_number]
        owner_position = block_number // blk_dev
        distance = (sta_position - owner_position) % sta_count
        held = lax.dynamic_index_in_dim(candidates, distance, 0, keepdims=False)
        sources = lax.dynamic_slice_in_dim(
            held, (block_number % blk_dev) * half_sources, half_sources, 3
        )
        cross_spectra = cross_terms(sources, receivers)
        correlated = lax.dot_general(
            lag_weights,
            cross_spectra,
            (((1, 2), (0, 1)), ((), ())),
            preferred_element_type=jnp.float32,
        )
        mask_row = pair_mask[block_number].astype(jnp.float32)
        allowed = jnp.sum(block_onehot * mask_row[None, :], axis=1)
        source_ids = (
            block_number * SRC
            + seg_position * half_sources
            + jnp.arange(half_sources, dtype=jnp.int32)
        )
        keep_pairs = (source_ids[:, None] != receiver_ids[None, :]).astype(jnp.float32) * allowed[
            None, :
        ]
        results.append((correlated * keep_pairs[None]).astype(jnp.bfloat16))
    return jnp.stack(results, 0)


def solution(mesh):
    return jax.shard_map(
        local,
        mesh=mesh,
        in_specs=(P("seg", None, "band", ("groups", "sta")), P("groups"), P("groups", None)),
        out_specs=P(None, "band", "seg", ("groups", "sta")),
        check_vma=False,
    )
```

```python
import math

import jax
import jax.numpy as jnp
from jax import lax
from jax.sharding import PartitionSpec as P

SEGS = 8
STEPS = 2
SRC = 128
BLK_DEV = 1
BAND_BINS = 256
HALF = 64
LAGS = 128


EPSILON = 1e-06


def padded(cells, sides, width):
    for axis, dim in sides:
        count = lax.axis_size(axis)
        ends = count - 1
        head = lax.slice_in_dim(cells, 0, width, axis=dim)
        tail = lax.slice_in_dim(cells, cells.shape[dim] - width, cells.shape[dim], axis=dim)
        if count == 2:
            first = lax.axis_index(axis) == 0
            swapped = lax.ppermute(jnp.where(first, tail, head), axis, [(0, 1), (1, 0)])
            zeros = jnp.zeros_like(swapped)
            lower = jnp.where(first, zeros, swapped)
            upper = jnp.where(first, swapped, zeros)
        else:
            lower = lax.ppermute(tail, axis, [(i, (i + 1) % count) for i in range(ends)])
            upper = lax.ppermute(head, axis, [((i + 1) % count, i) for i in range(ends)])
        cells = jnp.concatenate([lower, cells, upper], axis=dim)
    return cells


def from_root(block, axis, source):
    block = jnp.where(lax.axis_index(axis) == source, block, jnp.zeros_like(block))
    return lax.psum(block, axis)


def lag_table(first_bin):
    bin_number = first_bin + jnp.arange(BAND_BINS, dtype=jnp.int32)
    lag_number = jnp.arange(LAGS, dtype=jnp.int32) - LAGS // 2
    phase_steps = jnp.remainder(lag_number[:, None] * bin_number[None, :], 2 * BAND_BINS)
    phases = phase_steps.astype(jnp.float32) * (math.pi / BAND_BINS)
    normalizer = 1.0 / math.sqrt(SEGS * BAND_BINS)
    weights = jnp.stack([jnp.cos(phases), -jnp.sin(phases)], axis=2) * normalizer
    return weights.astype(jnp.bfloat16).reshape(LAGS, 2 * BAND_BINS)


def cross_terms(sources, receivers):
    src_real = sources[:, 0]
    src_imag = sources[:, 1]
    left_stack = jnp.stack(
        [jnp.concatenate([src_real, src_imag], 0), jnp.concatenate([src_imag, -src_real], 0)], 0
    )
    right_stack = jnp.concatenate([receivers[:, 0], receivers[:, 1]], 0)
    cross_spectra = jnp.einsum(
        "ctfs,tfn->fcsn", left_stack, right_stack, preferred_element_type=jnp.float32
    )
    return cross_spectra.astype(jnp.bfloat16)


def local(spectra, plan, pair_mask):
    seg_local = spectra.shape[0]
    band_bins = spectra.shape[2]
    sta_local = spectra.shape[3]
    band_position = lax.axis_index("band")
    sta_position = lax.axis_index("sta")
    seg_position = lax.axis_index("seg")
    total_bins = band_bins * lax.axis_size("band")
    half_sources = SRC // lax.axis_size("seg")
    amplitude = jnp.sqrt(spectra[:, 0] ** 2 + spectra[:, 1] ** 2)
    extended = padded(amplitude, (("band", 1),), HALF)
    block_width = 2 * HALF
    block_count = band_bins // block_width
    lower_part = extended[:, : block_count * block_width].reshape(
        seg_local, block_count, block_width, sta_local
    )
    upper_part = extended[:, block_width:].reshape(seg_local, block_count, block_width, sta_local)
    windows = jnp.concatenate([lower_part, upper_part], axis=2)
    offsets = jnp.arange(2 * block_width, dtype=jnp.int32)[:, None]
    targets = jnp.arange(block_width, dtype=jnp.int32)[None, :]
    band_matrix = ((offsets >= targets) & (offsets <= targets + 2 * HALF)).astype(jnp.float32)
    window_sums = jnp.einsum("tbgn,gf->tbfn", windows, band_matrix, precision=lax.Precision.HIGHEST)
    window_sums = window_sums.reshape(seg_local, band_bins, sta_local)
    bin_number = band_position * band_bins + jnp.arange(band_bins, dtype=jnp.int32)
    in_range = (
        jnp.minimum(bin_number + HALF, total_bins - 1) - jnp.maximum(bin_number - HALF, 0) + 1
    ).astype(jnp.float32)
    smooth = window_sums / in_range[None, :, None]
    white = (spectra / (smooth[:, None] + EPSILON)).astype(jnp.bfloat16)
    seg_count = lax.axis_size("seg")
    sta_count = lax.axis_size("sta")
    receivers = lax.all_gather(white, "seg", axis=0, tiled=True) if seg_count > 2 else None
    if receivers is None:
        partner = lax.ppermute(white, "seg", [(0, 1), (1, 0)])
        receivers = jnp.where(
            seg_position == 0,
            jnp.concatenate([white, partner], 0),
            jnp.concatenate([partner, white], 0),
        )
    own_half = lax.dynamic_slice_in_dim(receivers, seg_position * half_sources, half_sources, 3)
    shifted = [own_half]
    for shift in range(1, sta_count):
        shifted.append(
            lax.ppermute(own_half, "sta", [(i, (i + shift) % sta_count) for i in range(sta_count)])
        )
    blk_dev = sta_local // SRC
    lag_weights = lag_table(band_position * band_bins).reshape(LAGS, band_bins, 2)
    receiver_ids = sta_position * sta_local + jnp.arange(sta_local, dtype=jnp.int32)
    block_columns = jnp.arange(pair_mask.shape[1], dtype=jnp.int32)
    block_onehot = ((receiver_ids // SRC)[:, None] == block_columns[None, :]).astype(jnp.float32)
    chosen = []
    for step_number in range(STEPS):
        owner_position = plan[step_number] // blk_dev
        distance = (sta_position - owner_position) % sta_count
        sources = shifted[0]
        for shift in range(1, sta_count):
            sources = jnp.where(distance == shift, shifted[shift], sources)
        chosen.append(sources)
    sources = jnp.concatenate(chosen, 3)
    cross_spectra = cross_terms(sources, receivers)
    correlated = lax.dot_general(
        lag_weights,
        cross_spectra,
        (((1, 2), (0, 1)), ((), ())),
        preferred_element_type=jnp.float32,
    )
    results = []
    for step_number in range(STEPS):
        block_number = plan[step_number]
        mask_row = pair_mask[block_number].astype(jnp.float32)
        allowed = jnp.sum(block_onehot * mask_row[None, :], axis=1)
        source_ids = (
            block_number * SRC
            + seg_position * half_sources
            + jnp.arange(half_sources, dtype=jnp.int32)
        )
        keep_pairs = (source_ids[:, None] != receiver_ids[None, :]).astype(jnp.float32) * allowed[
            None, :
        ]
        part = lax.slice_in_dim(correlated, step_number * half_sources, (step_number + 1) * half_sources, axis=1)
        results.append((part * keep_pairs[None]).astype(jnp.bfloat16))
    return jnp.stack(results, 0)


def solution(mesh):
    return jax.shard_map(
        local,
        mesh=mesh,
        in_specs=(P("seg", None, "band", ("groups", "sta")), P("groups"), P("groups", None)),
        out_specs=P(None, "band", "seg", ("groups", "sta")),
        check_vma=False,
    )
```

```python
import math

import jax
import jax.numpy as jnp
from jax import lax
from jax.sharding import PartitionSpec as P

SEGS = 8
STEPS = 2
SRC = 128
BLK_DEV = 1
BAND_BINS = 256
HALF = 64
LAGS = 128


EPSILON = 1e-06


def padded(cells, sides, width):
    for axis, dim in sides:
        count = lax.axis_size(axis)
        ends = count - 1
        head = lax.slice_in_dim(cells, 0, width, axis=dim)
        tail = lax.slice_in_dim(cells, cells.shape[dim] - width, cells.shape[dim], axis=dim)
        if count == 2:
            first = lax.axis_index(axis) == 0
            swapped = lax.ppermute(jnp.where(first, tail, head), axis, [(0, 1), (1, 0)])
            zeros = jnp.zeros_like(swapped)
            lower = jnp.where(first, zeros, swapped)
            upper = jnp.where(first, swapped, zeros)
        else:
            lower = lax.ppermute(tail, axis, [(i, (i + 1) % count) for i in range(ends)])
            upper = lax.ppermute(head, axis, [((i + 1) % count, i) for i in range(ends)])
        cells = jnp.concatenate([lower, cells, upper], axis=dim)
    return cells


def from_root(block, axis, source):
    block = jnp.where(lax.axis_index(axis) == source, block, jnp.zeros_like(block))
    return lax.psum(block, axis)


def lag_table(first_bin):
    bin_number = first_bin + jnp.arange(BAND_BINS, dtype=jnp.int32)
    lag_number = jnp.arange(LAGS, dtype=jnp.int32) - LAGS // 2
    phase_steps = jnp.remainder(lag_number[:, None] * bin_number[None, :], 2 * BAND_BINS)
    phases = phase_steps.astype(jnp.float32) * (math.pi / BAND_BINS)
    normalizer = 1.0 / math.sqrt(SEGS * BAND_BINS)
    weights = jnp.stack([jnp.cos(phases), -jnp.sin(phases)], axis=2) * normalizer
    return weights.astype(jnp.bfloat16).reshape(LAGS, 2 * BAND_BINS)


def cross_terms(sources, receivers):
    src_real = sources[:, 0]
    src_imag = sources[:, 1]
    left_stack = jnp.stack(
        [jnp.concatenate([src_real, src_imag], 0), jnp.concatenate([src_imag, -src_real], 0)], 0
    )
    right_stack = jnp.concatenate([receivers[:, 0], receivers[:, 1]], 0)
    cross_spectra = jnp.einsum(
        "ctfs,tfn->fcsn", left_stack, right_stack, preferred_element_type=jnp.float32
    )
    return cross_spectra.astype(jnp.bfloat16)


def local(spectra, plan, pair_mask):
    seg_local = spectra.shape[0]
    band_bins = spectra.shape[2]
    sta_local = spectra.shape[3]
    band_position = lax.axis_index("band")
    sta_position = lax.axis_index("sta")
    seg_position = lax.axis_index("seg")
    total_bins = band_bins * lax.axis_size("band")
    half_sources = SRC // lax.axis_size("seg")
    amplitude = jnp.sqrt(spectra[:, 0] ** 2 + spectra[:, 1] ** 2)
    extended = padded(amplitude, (("band", 1),), HALF)
    block_width = 2 * HALF
    block_count = band_bins // block_width
    lower_part = extended[:, : block_count * block_width].reshape(
        seg_local, block_count, block_width, sta_local
    )
    upper_part = extended[:, block_width:].reshape(seg_local, block_count, block_width, sta_local)
    windows = jnp.concatenate([lower_part, upper_part], axis=2)
    offsets = jnp.arange(2 * block_width, dtype=jnp.int32)[:, None]
    targets = jnp.arange(block_width, dtype=jnp.int32)[None, :]
    band_matrix = ((offsets >= targets) & (offsets <= targets + 2 * HALF)).astype(jnp.float32)
    window_sums = jnp.einsum("tbgn,gf->tbfn", windows, band_matrix, precision=lax.Precision.HIGHEST)
    window_sums = window_sums.reshape(seg_local, band_bins, sta_local)
    bin_number = band_position * band_bins + jnp.arange(band_bins, dtype=jnp.int32)
    in_range = (
        jnp.minimum(bin_number + HALF, total_bins - 1) - jnp.maximum(bin_number - HALF, 0) + 1
    ).astype(jnp.float32)
    smooth = window_sums / in_range[None, :, None]
    white = (spectra / (smooth[:, None] + EPSILON)).astype(jnp.bfloat16)
    seg_count = lax.axis_size("seg")
    sta_count = lax.axis_size("sta")
    receivers = lax.all_gather(white, "seg", axis=0, tiled=True) if seg_count > 2 else None
    if receivers is None:
        partner = lax.ppermute(white, "seg", [(0, 1), (1, 0)])
        receivers = jnp.where(
            seg_position == 0,
            jnp.concatenate([white, partner], 0),
            jnp.concatenate([partner, white], 0),
        )
    own_half = lax.dynamic_slice_in_dim(receivers, seg_position * half_sources, half_sources, 3)
    split = band_bins // 2
    gathered = lax.all_gather(own_half[:, :, :split], "sta", axis=0, tiled=False)
    upper = own_half[:, :, split:]
    shifted = [upper]
    for shift in range(1, sta_count):
        shifted.append(
            lax.ppermute(upper, "sta", [(i, (i + shift) % sta_count) for i in range(sta_count)])
        )
    candidates = jnp.stack(shifted, 0)
    blk_dev = sta_local // SRC
    lag_weights = lag_table(band_position * band_bins).reshape(LAGS, band_bins, 2)
    receiver_ids = sta_position * sta_local + jnp.arange(sta_local, dtype=jnp.int32)
    block_columns = jnp.arange(pair_mask.shape[1], dtype=jnp.int32)
    block_onehot = ((receiver_ids // SRC)[:, None] == block_columns[None, :]).astype(jnp.float32)
    results = []
    for step_number in range(STEPS):
        block_number = plan[step_number]
        owner_position = block_number // blk_dev
        distance = (sta_position - owner_position) % sta_count
        held = jnp.concatenate(
            [
                lax.dynamic_index_in_dim(gathered, owner_position, 0, keepdims=False),
                lax.dynamic_index_in_dim(candidates, distance, 0, keepdims=False),
            ],
            2,
        )
        sources = lax.dynamic_slice_in_dim(
            held, (block_number % blk_dev) * half_sources, half_sources, 3
        )
        cross_spectra = cross_terms(sources, receivers)
        correlated = lax.dot_general(
            lag_weights,
            cross_spectra,
            (((1, 2), (0, 1)), ((), ())),
            preferred_element_type=jnp.float32,
        )
        mask_row = pair_mask[block_number].astype(jnp.float32)
        allowed = jnp.sum(block_onehot * mask_row[None, :], axis=1)
        source_ids = (
            block_number * SRC
            + seg_position * half_sources
            + jnp.arange(half_sources, dtype=jnp.int32)
        )
        keep_pairs = (source_ids[:, None] != receiver_ids[None, :]).astype(jnp.float32) * allowed[
            None, :
        ]
        results.append((correlated * keep_pairs[None]).astype(jnp.bfloat16))
    return jnp.stack(results, 0)


def solution(mesh):
    return jax.shard_map(
        local,
        mesh=mesh,
        in_specs=(P("seg", None, "band", ("groups", "sta")), P("groups"), P("groups", None)),
        out_specs=P(None, "band", "seg", ("groups", "sta")),
        check_vma=False,
    )
```

```python
import math

import jax
import jax.numpy as jnp
from jax import lax
from jax.sharding import PartitionSpec as P


SEGS = 8
STEPS = 2
SRC = 128
BAND_BINS = 256
HALF = 64
LAGS = 128


EPSILON = 1e-06


def padded(cells, sides, width):
    for axis, dim in sides:
        count = lax.axis_size(axis)
        ends = count - 1
        head = lax.slice_in_dim(cells, 0, width, axis=dim)
        tail = lax.slice_in_dim(cells, cells.shape[dim] - width, cells.shape[dim], axis=dim)
        if count == 2:
            first = lax.axis_index(axis) == 0
            swapped = lax.ppermute(jnp.where(first, tail, head), axis, [(0, 1), (1, 0)])
            zeros = jnp.zeros_like(swapped)
            lower = jnp.where(first, zeros, swapped)
            upper = jnp.where(first, swapped, zeros)
        else:
            lower = lax.ppermute(tail, axis, [(i, (i + 1) % count) for i in range(ends)])
            upper = lax.ppermute(head, axis, [((i + 1) % count, i) for i in range(ends)])
        cells = jnp.concatenate([lower, cells, upper], axis=dim)
    return cells


def lag_table(first_bin):
    bin_number = first_bin + jnp.arange(BAND_BINS, dtype=jnp.int32)
    lag_number = jnp.arange(LAGS, dtype=jnp.int32) - LAGS // 2
    phase_steps = jnp.remainder(lag_number[:, None] * bin_number[None, :], 2 * BAND_BINS)
    phases = phase_steps.astype(jnp.float32) * (math.pi / BAND_BINS)
    normalizer = 1.0 / math.sqrt(SEGS * BAND_BINS)
    weights = jnp.stack([jnp.cos(phases), -jnp.sin(phases)], axis=2) * normalizer
    return weights.astype(jnp.bfloat16).reshape(LAGS, 2 * BAND_BINS)


def cross_terms(sources, receivers):
    src_real = sources[:, 0]
    src_imag = sources[:, 1]
    left_stack = jnp.stack(
        [jnp.concatenate([src_real, src_imag], 0), jnp.concatenate([src_imag, -src_real], 0)], 0
    )
    right_stack = jnp.concatenate([receivers[:, 0], receivers[:, 1]], 0)
    cross_spectra = jnp.einsum(
        "ctfs,tfn->fcsn", left_stack, right_stack, preferred_element_type=jnp.float32
    )
    return cross_spectra.astype(jnp.bfloat16)


def local(spectra, plan, pair_mask):
    seg_local = spectra.shape[0]
    band_bins = spectra.shape[2]
    sta_local = spectra.shape[3]
    band_position = lax.axis_index("band")
    sta_position = lax.axis_index("sta")
    seg_position = lax.axis_index("seg")
    total_bins = band_bins * lax.axis_size("band")
    half_sources = SRC // lax.axis_size("seg")
    amplitude = jnp.sqrt(spectra[:, 0] ** 2 + spectra[:, 1] ** 2)
    seg_count = lax.axis_size("seg")
    sta_count = lax.axis_size("sta")
    bin_number = band_position * band_bins + jnp.arange(band_bins, dtype=jnp.int32)
    in_range = (
        jnp.minimum(bin_number + HALF, total_bins - 1) - jnp.maximum(bin_number - HALF, 0) + 1
    ).astype(jnp.float32)

    def whiten_from(extended, spectra):
        block_width = 2 * HALF
        block_count = band_bins // block_width
        lower_part = extended[:, : block_count * block_width].reshape(
            seg_local, block_count, block_width, sta_local
        )
        upper_part = extended[:, block_width:].reshape(
            seg_local, block_count, block_width, sta_local
        )
        windows = jnp.concatenate([lower_part, upper_part], axis=2)
        offsets = jnp.arange(2 * block_width, dtype=jnp.int32)[:, None]
        targets = jnp.arange(block_width, dtype=jnp.int32)[None, :]
        band_matrix = ((offsets >= targets) & (offsets <= targets + 2 * HALF)).astype(jnp.float32)
        window_sums = jnp.einsum(
            "tbgn,gf->tbfn", windows, band_matrix, precision=lax.Precision.HIGHEST
        )
        window_sums = window_sums.reshape(seg_local, band_bins, sta_local)
        smooth = window_sums / in_range[None, :, None]
        return (spectra / (smooth[:, None] + EPSILON)).astype(jnp.bfloat16)

    def spread(white):
        partner = lax.ppermute(white, "seg", [(0, 1), (1, 0)])
        receivers = jnp.where(
            seg_position == 0,
            jnp.concatenate([white, partner], 0),
            jnp.concatenate([partner, white], 0),
        )
        own_half = lax.dynamic_slice_in_dim(
            receivers, seg_position * half_sources, half_sources, 3
        )
        shifted = [own_half]
        for shift in range(1, sta_count):
            shifted.append(
                lax.ppermute(
                    own_half, "sta", [(i, (i + shift) % sta_count) for i in range(sta_count)]
                )
            )
        return receivers, jnp.stack(shifted, 0)

    split_bins = seg_count == 2 and band_bins == 4 * HALF
    if split_bins:
        rim = jnp.zeros((seg_local, HALF, sta_local), amplitude.dtype)
        inner_amplitude, inner_spectra = lax.optimization_barrier((amplitude, spectra))
        inner = whiten_from(jnp.concatenate([rim, inner_amplitude, rim], 1), inner_spectra)
        inner = lax.optimization_barrier(inner[:, :, HALF:-HALF])
        halo_amplitude, _ = lax.optimization_barrier((amplitude, inner))
        extended = padded(halo_amplitude, (("band", 1),), HALF)
        outer = whiten_from(extended, spectra)
        outer = jnp.concatenate([outer[:, :, :HALF], outer[:, :, -HALF:]], 2)
        inner_receivers, inner_candidates = spread(inner)
        outer_receivers, outer_candidates = spread(outer)

        def by_bins(inner_part, outer_part):
            return jnp.concatenate(
                [outer_part[..., :HALF, :], inner_part, outer_part[..., HALF:, :]], -2
            )

        receivers = by_bins(inner_receivers, outer_receivers)
        candidates = by_bins(inner_candidates, outer_candidates)
    else:
        white = whiten_from(padded(amplitude, (("band", 1),), HALF), spectra)
        if seg_count == 2:
            receivers, candidates = spread(white)
        else:
            receivers = lax.all_gather(white, "seg", axis=0, tiled=True)
            own_half = lax.dynamic_slice_in_dim(
                receivers, seg_position * half_sources, half_sources, 3
            )
            shifted = [own_half]
            for shift in range(1, sta_count):
                shifted.append(
                    lax.ppermute(
                        own_half, "sta", [(i, (i + shift) % sta_count) for i in range(sta_count)]
                    )
                )
            candidates = jnp.stack(shifted, 0)
    blk_dev = sta_local // SRC
    lag_weights = lag_table(band_position * band_bins).reshape(LAGS, band_bins, 2)
    receiver_ids = sta_position * sta_local + jnp.arange(sta_local, dtype=jnp.int32)
    block_columns = jnp.arange(pair_mask.shape[1], dtype=jnp.int32)
    block_onehot = ((receiver_ids // SRC)[:, None] == block_columns[None, :]).astype(jnp.float32)
    results = []
    for step_number in range(STEPS):
        block_number = plan[step_number]
        owner_position = block_number // blk_dev
        distance = (sta_position - owner_position) % sta_count
        held = lax.dynamic_index_in_dim(candidates, distance, 0, keepdims=False)
        sources = lax.dynamic_slice_in_dim(
            held, (block_number % blk_dev) * half_sources, half_sources, 3
        )
        cross_spectra = cross_terms(sources, receivers)
        correlated = lax.dot_general(
            lag_weights,
            cross_spectra,
            (((1, 2), (0, 1)), ((), ())),
            preferred_element_type=jnp.float32,
        )
        mask_row = pair_mask[block_number].astype(jnp.float32)
        allowed = jnp.sum(block_onehot * mask_row[None, :], axis=1)
        source_ids = (
            block_number * SRC
            + seg_position * half_sources
            + jnp.arange(half_sources, dtype=jnp.int32)
        )
        keep_pairs = (source_ids[:, None] != receiver_ids[None, :]).astype(jnp.float32) * allowed[
            None, :
        ]
        results.append((correlated * keep_pairs[None]).astype(jnp.bfloat16))
    return jnp.stack(results, 0)


def solution(mesh):
    return jax.shard_map(
        local,
        mesh=mesh,
        in_specs=(P("seg", None, "band", ("groups", "sta")), P("groups"), P("groups", None)),
        out_specs=P(None, "band", "seg", ("groups", "sta")),
        check_vma=False,
    )
```

```python
import math

import jax
import jax.numpy as jnp
from jax import lax
from jax.sharding import PartitionSpec as P

SEGS = 8
STEPS = 2
SRC = 128
BLK_DEV = 1
BAND_BINS = 256
HALF = 64
LAGS = 128


EPSILON = 1e-06


def padded(cells, sides, width):
    for axis, dim in sides:
        count = lax.axis_size(axis)
        ends = count - 1
        head = lax.slice_in_dim(cells, 0, width, axis=dim)
        tail = lax.slice_in_dim(cells, cells.shape[dim] - width, cells.shape[dim], axis=dim)
        if count == 2:
            first = lax.axis_index(axis) == 0
            swapped = lax.ppermute(jnp.where(first, tail, head), axis, [(0, 1), (1, 0)])
            zeros = jnp.zeros_like(swapped)
            lower = jnp.where(first, zeros, swapped)
            upper = jnp.where(first, swapped, zeros)
        else:
            lower = lax.ppermute(tail, axis, [(i, (i + 1) % count) for i in range(ends)])
            upper = lax.ppermute(head, axis, [((i + 1) % count, i) for i in range(ends)])
        cells = jnp.concatenate([lower, cells, upper], axis=dim)
    return cells


def from_root(block, axis, source):
    block = jnp.where(lax.axis_index(axis) == source, block, jnp.zeros_like(block))
    return lax.psum(block, axis)


def lag_table(first_bin):
    bin_number = first_bin + jnp.arange(BAND_BINS, dtype=jnp.int32)
    lag_number = jnp.arange(LAGS, dtype=jnp.int32) - LAGS // 2
    phase_steps = jnp.remainder(lag_number[:, None] * bin_number[None, :], 2 * BAND_BINS)
    phases = phase_steps.astype(jnp.float32) * (math.pi / BAND_BINS)
    normalizer = 1.0 / math.sqrt(SEGS * BAND_BINS)
    weights = jnp.stack([jnp.cos(phases), -jnp.sin(phases)], axis=2) * normalizer
    return weights.astype(jnp.bfloat16).reshape(LAGS, 2 * BAND_BINS)


def cross_terms(sources, receivers):
    src_real = sources[:, 0]
    src_imag = sources[:, 1]
    left_stack = jnp.stack(
        [jnp.concatenate([src_real, src_imag], 0), jnp.concatenate([src_imag, -src_real], 0)], 0
    )
    right_stack = jnp.concatenate([receivers[:, 0], receivers[:, 1]], 0)
    cross_spectra = jnp.einsum(
        "ctfs,tfn->fcsn", left_stack, right_stack, preferred_element_type=jnp.float32
    )
    return cross_spectra.astype(jnp.bfloat16)


def local(spectra, plan, pair_mask):
    seg_local = spectra.shape[0]
    band_bins = spectra.shape[2]
    sta_local = spectra.shape[3]
    band_position = lax.axis_index("band")
    sta_position = lax.axis_index("sta")
    seg_position = lax.axis_index("seg")
    total_bins = band_bins * lax.axis_size("band")
    half_sources = SRC // lax.axis_size("seg")
    amplitude = jnp.sqrt(spectra[:, 0] ** 2 + spectra[:, 1] ** 2)
    extended = padded(amplitude, (("band", 1),), HALF)
    block_width = 2 * HALF
    block_count = band_bins // block_width
    lower_part = extended[:, : block_count * block_width].reshape(
        seg_local, block_count, block_width, sta_local
    )
    upper_part = extended[:, block_width:].reshape(seg_local, block_count, block_width, sta_local)
    windows = jnp.concatenate([lower_part, upper_part], axis=2)
    offsets = jnp.arange(2 * block_width, dtype=jnp.int32)[:, None]
    targets = jnp.arange(block_width, dtype=jnp.int32)[None, :]
    band_matrix = ((offsets >= targets) & (offsets <= targets + 2 * HALF)).astype(jnp.float32)
    window_sums = jnp.einsum("tbgn,gf->tbfn", windows, band_matrix, precision=lax.Precision.HIGHEST)
    window_sums = window_sums.reshape(seg_local, band_bins, sta_local)
    bin_number = band_position * band_bins + jnp.arange(band_bins, dtype=jnp.int32)
    in_range = (
        jnp.minimum(bin_number + HALF, total_bins - 1) - jnp.maximum(bin_number - HALF, 0) + 1
    ).astype(jnp.float32)
    smooth = window_sums / in_range[None, :, None]
    white = (spectra / (smooth[:, None] + EPSILON)).astype(jnp.bfloat16)
    seg_count = lax.axis_size("seg")
    sta_count = lax.axis_size("sta")
    receivers = lax.all_gather(white, "seg", axis=0, tiled=True) if seg_count > 2 else None
    if receivers is None:
        partner = lax.ppermute(white, "seg", [(0, 1), (1, 0)])
        receivers = jnp.where(
            seg_position == 0,
            jnp.concatenate([white, partner], 0),
            jnp.concatenate([partner, white], 0),
        )
    own_half = lax.dynamic_slice_in_dim(receivers, seg_position * half_sources, half_sources, 3)
    copies = jnp.broadcast_to(own_half[None], (sta_count,) + own_half.shape)
    candidates = lax.all_to_all(copies, "sta", 0, 0, tiled=True)
    blk_dev = sta_local // SRC
    lag_weights = lag_table(band_position * band_bins).reshape(LAGS, band_bins, 2)
    receiver_ids = sta_position * sta_local + jnp.arange(sta_local, dtype=jnp.int32)
    block_columns = jnp.arange(pair_mask.shape[1], dtype=jnp.int32)
    block_onehot = ((receiver_ids // SRC)[:, None] == block_columns[None, :]).astype(jnp.float32)
    results = []
    for step_number in range(STEPS):
        block_number = plan[step_number]
        owner_position = block_number // blk_dev
        held = lax.dynamic_index_in_dim(candidates, owner_position, 0, keepdims=False)
        sources = lax.dynamic_slice_in_dim(
            held, (block_number % blk_dev) * half_sources, half_sources, 3
        )
        cross_spectra = cross_terms(sources, receivers)
        correlated = lax.dot_general(
            lag_weights,
            cross_spectra,
            (((1, 2), (0, 1)), ((), ())),
            preferred_element_type=jnp.float32,
        )
        mask_row = pair_mask[block_number].astype(jnp.float32)
        allowed = jnp.sum(block_onehot * mask_row[None, :], axis=1)
        source_ids = (
            block_number * SRC
            + seg_position * half_sources
            + jnp.arange(half_sources, dtype=jnp.int32)
        )
        keep_pairs = (source_ids[:, None] != receiver_ids[None, :]).astype(jnp.float32) * allowed[
            None, :
        ]
        results.append((correlated * keep_pairs[None]).astype(jnp.bfloat16))
    return jnp.stack(results, 0)


def solution(mesh):
    return jax.shard_map(
        local,
        mesh=mesh,
        in_specs=(P("seg", None, "band", ("groups", "sta")), P("groups"), P("groups", None)),
        out_specs=P(None, "band", "seg", ("groups", "sta")),
        check_vma=False,
    )
```

```python
import math

import jax
import jax.numpy as jnp
from jax import lax
from jax.sharding import PartitionSpec as P

SEGS = 8
STEPS = 2
SRC = 128
BLK_DEV = 1
BAND_BINS = 256
HALF = 64
LAGS = 128


EPSILON = 1e-06


def padded(cells, sides, width):
    for axis, dim in sides:
        count = lax.axis_size(axis)
        ends = count - 1
        head = lax.slice_in_dim(cells, 0, width, axis=dim)
        tail = lax.slice_in_dim(cells, cells.shape[dim] - width, cells.shape[dim], axis=dim)
        if count == 2:
            first = lax.axis_index(axis) == 0
            swapped = lax.ppermute(jnp.where(first, tail, head), axis, [(0, 1), (1, 0)])
            zeros = jnp.zeros_like(swapped)
            lower = jnp.where(first, zeros, swapped)
            upper = jnp.where(first, swapped, zeros)
        else:
            lower = lax.ppermute(tail, axis, [(i, (i + 1) % count) for i in range(ends)])
            upper = lax.ppermute(head, axis, [((i + 1) % count, i) for i in range(ends)])
        cells = jnp.concatenate([lower, cells, upper], axis=dim)
    return cells


def from_root(block, axis, source):
    block = jnp.where(lax.axis_index(axis) == source, block, jnp.zeros_like(block))
    return lax.psum(block, axis)


def lag_table(first_bin):
    bin_number = first_bin + jnp.arange(BAND_BINS, dtype=jnp.int32)
    lag_number = jnp.arange(LAGS, dtype=jnp.int32) - LAGS // 2
    phase_steps = jnp.remainder(lag_number[:, None] * bin_number[None, :], 2 * BAND_BINS)
    phases = phase_steps.astype(jnp.float32) * (math.pi / BAND_BINS)
    normalizer = 1.0 / math.sqrt(SEGS * BAND_BINS)
    weights = jnp.stack([jnp.cos(phases), -jnp.sin(phases)], axis=2) * normalizer
    return weights.astype(jnp.bfloat16).reshape(LAGS, 2 * BAND_BINS)


def cross_terms(sources, receivers):
    src_real = sources[:, 0]
    src_imag = sources[:, 1]
    left_stack = jnp.stack(
        [jnp.concatenate([src_real, src_imag], 0), jnp.concatenate([src_imag, -src_real], 0)], 0
    )
    right_stack = jnp.concatenate([receivers[:, 0], receivers[:, 1]], 0)
    cross_spectra = jnp.einsum(
        "ctfs,tfn->fcsn", left_stack, right_stack, preferred_element_type=jnp.float32
    )
    return cross_spectra.astype(jnp.bfloat16)


def local(spectra, plan, pair_mask):
    seg_local = spectra.shape[0]
    band_bins = spectra.shape[2]
    sta_local = spectra.shape[3]
    band_position = lax.axis_index("band")
    sta_position = lax.axis_index("sta")
    seg_position = lax.axis_index("seg")
    total_bins = band_bins * lax.axis_size("band")
    half_sources = SRC // lax.axis_size("seg")
    amplitude = jnp.sqrt(spectra[:, 0] ** 2 + spectra[:, 1] ** 2)
    extended = padded(amplitude, (("band", 1),), HALF)
    block_width = 2 * HALF
    block_count = band_bins // block_width
    lower_part = extended[:, : block_count * block_width].reshape(
        seg_local, block_count, block_width, sta_local
    )
    upper_part = extended[:, block_width:].reshape(seg_local, block_count, block_width, sta_local)
    windows = jnp.concatenate([lower_part, upper_part], axis=2)
    offsets = jnp.arange(2 * block_width, dtype=jnp.int32)[:, None]
    targets = jnp.arange(block_width, dtype=jnp.int32)[None, :]
    band_matrix = ((offsets >= targets) & (offsets <= targets + 2 * HALF)).astype(jnp.float32)
    window_sums = jnp.einsum("tbgn,gf->tbfn", windows, band_matrix, precision=lax.Precision.HIGHEST)
    window_sums = window_sums.reshape(seg_local, band_bins, sta_local)
    bin_number = band_position * band_bins + jnp.arange(band_bins, dtype=jnp.int32)
    in_range = (
        jnp.minimum(bin_number + HALF, total_bins - 1) - jnp.maximum(bin_number - HALF, 0) + 1
    ).astype(jnp.float32)
    smooth = window_sums / in_range[None, :, None]
    white = (spectra / (smooth[:, None] + EPSILON)).astype(jnp.bfloat16)
    seg_count = lax.axis_size("seg")
    sta_count = lax.axis_size("sta")
    receivers = lax.all_gather(white, "seg", axis=0, tiled=True) if seg_count > 2 else None
    if receivers is None:
        partner = lax.ppermute(white, "seg", [(0, 1), (1, 0)])
        receivers = jnp.concatenate([white, partner], 0)
    own_half = lax.dynamic_slice_in_dim(receivers, seg_position * half_sources, half_sources, 3)
    shifted = [own_half]
    for shift in range(1, sta_count):
        shifted.append(
            lax.ppermute(own_half, "sta", [(i, (i + shift) % sta_count) for i in range(sta_count)])
        )
    blk_dev = sta_local // SRC
    lag_weights = lag_table(band_position * band_bins).reshape(LAGS, band_bins, 2)
    receiver_ids = sta_position * sta_local + jnp.arange(sta_local, dtype=jnp.int32)
    block_columns = jnp.arange(pair_mask.shape[1], dtype=jnp.int32)
    block_onehot = ((receiver_ids // SRC)[:, None] == block_columns[None, :]).astype(jnp.float32)
    results = []
    for step_number in range(STEPS):
        block_number = plan[step_number]
        owner_position = block_number // blk_dev
        distance = (sta_position - owner_position) % sta_count
        held = lax.switch(distance, [lambda x=x: x for x in shifted])
        sources = lax.dynamic_slice_in_dim(
            held, (block_number % blk_dev) * half_sources, half_sources, 3
        )
        cross_spectra = cross_terms(sources, receivers)
        correlated = lax.dot_general(
            lag_weights,
            cross_spectra,
            (((1, 2), (0, 1)), ((), ())),
            preferred_element_type=jnp.float32,
        )
        mask_row = pair_mask[block_number].astype(jnp.float32)
        allowed = jnp.sum(block_onehot * mask_row[None, :], axis=1)
        source_ids = (
            block_number * SRC
            + seg_position * half_sources
            + jnp.arange(half_sources, dtype=jnp.int32)
        )
        keep_pairs = (source_ids[:, None] != receiver_ids[None, :]).astype(jnp.float32) * allowed[
            None, :
        ]
        results.append((correlated * keep_pairs[None]).astype(jnp.bfloat16))
    return jnp.stack(results, 0)


def solution(mesh):
    return jax.shard_map(
        local,
        mesh=mesh,
        in_specs=(P("seg", None, "band", ("groups", "sta")), P("groups"), P("groups", None)),
        out_specs=P(None, "band", "seg", ("groups", "sta")),
        check_vma=False,
    )
```

```python
import math

import jax
import jax.numpy as jnp
from jax import lax
from jax.sharding import PartitionSpec as P

SEGS = 8
STEPS = 2
SRC = 128
BLK_DEV = 1
BAND_BINS = 256
HALF = 64
LAGS = 128


EPSILON = 1e-06


def padded(cells, sides, width):
    for axis, dim in sides:
        count = lax.axis_size(axis)
        ends = count - 1
        head = lax.slice_in_dim(cells, 0, width, axis=dim)
        tail = lax.slice_in_dim(cells, cells.shape[dim] - width, cells.shape[dim], axis=dim)
        if count == 2:
            first = lax.axis_index(axis) == 0
            swapped = lax.ppermute(jnp.where(first, tail, head), axis, [(0, 1), (1, 0)])
            zeros = jnp.zeros_like(swapped)
            lower = jnp.where(first, zeros, swapped)
            upper = jnp.where(first, swapped, zeros)
        else:
            lower = lax.ppermute(tail, axis, [(i, (i + 1) % count) for i in range(ends)])
            upper = lax.ppermute(head, axis, [((i + 1) % count, i) for i in range(ends)])
        cells = jnp.concatenate([lower, cells, upper], axis=dim)
    return cells


def from_root(block, axis, source):
    block = jnp.where(lax.axis_index(axis) == source, block, jnp.zeros_like(block))
    return lax.psum(block, axis)


def lag_table(first_bin):
    bin_number = first_bin + jnp.arange(BAND_BINS, dtype=jnp.int32)
    lag_number = jnp.arange(LAGS, dtype=jnp.int32) - LAGS // 2
    phase_steps = jnp.remainder(lag_number[:, None] * bin_number[None, :], 2 * BAND_BINS)
    phases = phase_steps.astype(jnp.float32) * (math.pi / BAND_BINS)
    normalizer = 1.0 / math.sqrt(SEGS * BAND_BINS)
    weights = jnp.stack([jnp.cos(phases), -jnp.sin(phases)], axis=2) * normalizer
    return weights.astype(jnp.bfloat16).reshape(LAGS, 2 * BAND_BINS)


def cross_terms(sources, receivers):
    src_real = sources[:, 0]
    src_imag = sources[:, 1]
    left_stack = jnp.stack(
        [jnp.concatenate([src_real, src_imag], 0), jnp.concatenate([src_imag, -src_real], 0)], 0
    )
    right_stack = jnp.concatenate([receivers[:, 0], receivers[:, 1]], 0)
    cross_spectra = jnp.einsum(
        "ctfs,tfn->fcsn", left_stack, right_stack, preferred_element_type=jnp.float32
    )
    return cross_spectra.astype(jnp.bfloat16)


def local(spectra, plan, pair_mask):
    seg_local = spectra.shape[0]
    band_bins = spectra.shape[2]
    sta_local = spectra.shape[3]
    band_position = lax.axis_index("band")
    sta_position = lax.axis_index("sta")
    seg_position = lax.axis_index("seg")
    total_bins = band_bins * lax.axis_size("band")
    half_sources = SRC // lax.axis_size("seg")
    amplitude = jnp.sqrt(spectra[:, 0] ** 2 + spectra[:, 1] ** 2)
    extended = padded(amplitude, (("band", 1),), HALF)
    block_width = 2 * HALF
    block_count = band_bins // block_width
    lower_part = extended[:, : block_count * block_width].reshape(
        seg_local, block_count, block_width, sta_local
    )
    upper_part = extended[:, block_width:].reshape(seg_local, block_count, block_width, sta_local)
    windows = jnp.concatenate([lower_part, upper_part], axis=2)
    offsets = jnp.arange(2 * block_width, dtype=jnp.int32)[:, None]
    targets = jnp.arange(block_width, dtype=jnp.int32)[None, :]
    band_matrix = ((offsets >= targets) & (offsets <= targets + 2 * HALF)).astype(jnp.float32)
    window_sums = jnp.einsum("tbgn,gf->tbfn", windows, band_matrix, precision=lax.Precision.HIGHEST)
    window_sums = window_sums.reshape(seg_local, band_bins, sta_local)
    bin_number = band_position * band_bins + jnp.arange(band_bins, dtype=jnp.int32)
    in_range = (
        jnp.minimum(bin_number + HALF, total_bins - 1) - jnp.maximum(bin_number - HALF, 0) + 1
    ).astype(jnp.float32)
    smooth = window_sums / in_range[None, :, None]
    white = (spectra / (smooth[:, None] + EPSILON)).astype(jnp.bfloat16)
    seg_count = lax.axis_size("seg")
    sta_count = lax.axis_size("sta")
    if seg_count == 2:
        mine = lax.dynamic_slice_in_dim(white, seg_position * half_sources, half_sources, 3)
        theirs = lax.dynamic_slice_in_dim(
            white, (1 - seg_position) * half_sources, half_sources, 3
        )
        wanted = lax.ppermute(theirs, "seg", [(0, 1), (1, 0)])
        own_half = jnp.concatenate([mine, wanted], 0)
        kept = lax.ppermute(mine, "seg", [(0, 1), (1, 0)])
        partner = jnp.where(
            seg_position == 0,
            jnp.concatenate([wanted, kept], 3),
            jnp.concatenate([kept, wanted], 3),
        )
        receivers = jnp.concatenate([white, partner], 0)
    else:
        receivers = lax.all_gather(white, "seg", axis=0, tiled=True)
        own_half = lax.dynamic_slice_in_dim(
            receivers, seg_position * half_sources, half_sources, 3
        )
    shifted = [own_half]
    for shift in range(1, sta_count):
        shifted.append(
            lax.ppermute(own_half, "sta", [(i, (i + shift) % sta_count) for i in range(sta_count)])
        )
    candidates = jnp.stack(shifted, 0)
    blk_dev = sta_local // SRC
    lag_weights = lag_table(band_position * band_bins).reshape(LAGS, band_bins, 2)
    receiver_ids = sta_position * sta_local + jnp.arange(sta_local, dtype=jnp.int32)
    block_columns = jnp.arange(pair_mask.shape[1], dtype=jnp.int32)
    block_onehot = ((receiver_ids // SRC)[:, None] == block_columns[None, :]).astype(jnp.float32)
    results = []
    for step_number in range(STEPS):
        block_number = plan[step_number]
        owner_position = block_number // blk_dev
        distance = (sta_position - owner_position) % sta_count
        held = lax.dynamic_index_in_dim(candidates, distance, 0, keepdims=False)
        sources = lax.dynamic_slice_in_dim(
            held, (block_number % blk_dev) * half_sources, half_sources, 3
        )
        cross_spectra = cross_terms(sources, receivers)
        correlated = lax.dot_general(
            lag_weights,
            cross_spectra,
            (((1, 2), (0, 1)), ((), ())),
            preferred_element_type=jnp.float32,
        )
        mask_row = pair_mask[block_number].astype(jnp.float32)
        allowed = jnp.sum(block_onehot * mask_row[None, :], axis=1)
        source_ids = (
            block_number * SRC
            + seg_position * half_sources
            + jnp.arange(half_sources, dtype=jnp.int32)
        )
        keep_pairs = (source_ids[:, None] != receiver_ids[None, :]).astype(jnp.float32) * allowed[
            None, :
        ]
        results.append((correlated * keep_pairs[None]).astype(jnp.bfloat16))
    return jnp.stack(results, 0)


def solution(mesh):
    return jax.shard_map(
        local,
        mesh=mesh,
        in_specs=(P("seg", None, "band", ("groups", "sta")), P("groups"), P("groups", None)),
        out_specs=P(None, "band", "seg", ("groups", "sta")),
        check_vma=False,
    )
```

```python
import math

import jax
import jax.numpy as jnp
from jax import lax
from jax.sharding import PartitionSpec as P

SEGS = 8
STEPS = 2
SRC = 128
BLK_DEV = 1
BAND_BINS = 256
HALF = 64
LAGS = 128


EPSILON = 1e-06


def padded(cells, sides, width):
    for axis, dim in sides:
        count = lax.axis_size(axis)
        ends = count - 1
        head = lax.slice_in_dim(cells, 0, width, axis=dim)
        tail = lax.slice_in_dim(cells, cells.shape[dim] - width, cells.shape[dim], axis=dim)
        if count == 2:
            first = lax.axis_index(axis) == 0
            swapped = lax.ppermute(jnp.where(first, tail, head), axis, [(0, 1), (1, 0)])
            zeros = jnp.zeros_like(swapped)
            lower = jnp.where(first, zeros, swapped)
            upper = jnp.where(first, swapped, zeros)
        else:
            lower = lax.ppermute(tail, axis, [(i, (i + 1) % count) for i in range(ends)])
            upper = lax.ppermute(head, axis, [((i + 1) % count, i) for i in range(ends)])
        cells = jnp.concatenate([lower, cells, upper], axis=dim)
    return cells


def from_root(block, axis, source):
    block = jnp.where(lax.axis_index(axis) == source, block, jnp.zeros_like(block))
    return lax.psum(block, axis)


def lag_table(first_bin):
    bin_number = first_bin + jnp.arange(BAND_BINS, dtype=jnp.int32)
    lag_number = jnp.arange(LAGS, dtype=jnp.int32) - LAGS // 2
    phase_steps = jnp.remainder(lag_number[:, None] * bin_number[None, :], 2 * BAND_BINS)
    phases = phase_steps.astype(jnp.float32) * (math.pi / BAND_BINS)
    normalizer = 1.0 / math.sqrt(SEGS * BAND_BINS)
    weights = jnp.stack([jnp.cos(phases), -jnp.sin(phases)], axis=2) * normalizer
    return weights.astype(jnp.bfloat16).reshape(LAGS, 2 * BAND_BINS)


def cross_terms(sources, receivers):
    src_real = sources[:, 0]
    src_imag = sources[:, 1]
    left_stack = jnp.stack(
        [jnp.concatenate([src_real, src_imag], 0), jnp.concatenate([src_imag, -src_real], 0)], 0
    )
    right_stack = jnp.concatenate([receivers[:, 0], receivers[:, 1]], 0)
    cross_spectra = jnp.einsum(
        "ctfs,tfn->fcsn", left_stack, right_stack, preferred_element_type=jnp.float32
    )
    return cross_spectra.astype(jnp.bfloat16)


def local(spectra, plan, pair_mask):
    seg_local = spectra.shape[0]
    band_bins = spectra.shape[2]
    sta_local = spectra.shape[3]
    band_position = lax.axis_index("band")
    sta_position = lax.axis_index("sta")
    seg_position = lax.axis_index("seg")
    total_bins = band_bins * lax.axis_size("band")
    half_sources = SRC // lax.axis_size("seg")
    amplitude = jnp.sqrt(spectra[:, 0] ** 2 + spectra[:, 1] ** 2)
    extended = padded(amplitude, (("band", 1),), HALF)
    block_width = 2 * HALF
    block_count = band_bins // block_width
    lower_part = extended[:, : block_count * block_width].reshape(
        seg_local, block_count, block_width, sta_local
    )
    upper_part = extended[:, block_width:].reshape(seg_local, block_count, block_width, sta_local)
    windows = jnp.concatenate([lower_part, upper_part], axis=2)
    offsets = jnp.arange(2 * block_width, dtype=jnp.int32)[:, None]
    targets = jnp.arange(block_width, dtype=jnp.int32)[None, :]
    band_matrix = ((offsets >= targets) & (offsets <= targets + 2 * HALF)).astype(jnp.float32)
    window_sums = jnp.einsum("tbgn,gf->tbfn", windows, band_matrix, precision=lax.Precision.HIGHEST)
    window_sums = window_sums.reshape(seg_local, band_bins, sta_local)
    bin_number = band_position * band_bins + jnp.arange(band_bins, dtype=jnp.int32)
    in_range = (
        jnp.minimum(bin_number + HALF, total_bins - 1) - jnp.maximum(bin_number - HALF, 0) + 1
    ).astype(jnp.float32)
    smooth = window_sums / in_range[None, :, None]
    white = (spectra / (smooth[:, None] + EPSILON)).astype(jnp.bfloat16)
    seg_count = lax.axis_size("seg")
    sta_count = lax.axis_size("sta")
    receivers = lax.all_gather(white, "seg", axis=0, tiled=True) if seg_count > 2 else None
    if receivers is None:
        partner = lax.ppermute(white, "seg", [(0, 1), (1, 0)])
        receivers = jnp.where(
            seg_position == 0,
            jnp.concatenate([white, partner], 0),
            jnp.concatenate([partner, white], 0),
        )
    own_half = lax.dynamic_slice_in_dim(receivers, seg_position * half_sources, half_sources, 3)
    shifted = [own_half]
    for shift in range(1, sta_count):
        shifted.append(
            lax.ppermute(own_half, "sta", [(i, (i + shift) % sta_count) for i in range(sta_count)])
        )
    candidates = jnp.stack(shifted, 0)
    plan, pair_mask, _ = lax.optimization_barrier((plan, pair_mask, own_half))
    blk_dev = sta_local // SRC
    lag_weights = lag_table(band_position * band_bins).reshape(LAGS, band_bins, 2)
    receiver_ids = sta_position * sta_local + jnp.arange(sta_local, dtype=jnp.int32)
    block_columns = jnp.arange(pair_mask.shape[1], dtype=jnp.int32)
    block_onehot = ((receiver_ids // SRC)[:, None] == block_columns[None, :]).astype(jnp.float32)
    results = []
    for step_number in range(STEPS):
        block_number = plan[step_number]
        owner_position = block_number // blk_dev
        distance = (sta_position - owner_position) % sta_count
        held = lax.dynamic_index_in_dim(candidates, distance, 0, keepdims=False)
        sources = lax.dynamic_slice_in_dim(
            held, (block_number % blk_dev) * half_sources, half_sources, 3
        )
        cross_spectra = cross_terms(sources, receivers)
        correlated = lax.dot_general(
            lag_weights,
            cross_spectra,
            (((1, 2), (0, 1)), ((), ())),
            preferred_element_type=jnp.float32,
        )
        mask_row = pair_mask[block_number].astype(jnp.float32)
        allowed = jnp.sum(block_onehot * mask_row[None, :], axis=1)
        source_ids = (
            block_number * SRC
            + seg_position * half_sources
            + jnp.arange(half_sources, dtype=jnp.int32)
        )
        keep_pairs = (source_ids[:, None] != receiver_ids[None, :]).astype(jnp.float32) * allowed[
            None, :
        ]
        results.append((correlated * keep_pairs[None]).astype(jnp.bfloat16))
    return jnp.stack(results, 0)


def solution(mesh):
    return jax.shard_map(
        local,
        mesh=mesh,
        in_specs=(P("seg", None, "band", ("groups", "sta")), P("groups"), P("groups", None)),
        out_specs=P(None, "band", "seg", ("groups", "sta")),
        check_vma=False,
    )
```

```python
import math

import jax
import jax.numpy as jnp
from jax import lax
from jax.sharding import PartitionSpec as P


SEGS = 8
STEPS = 2
SRC = 128
BAND_BINS = 256
HALF = 64
LAGS = 128


EPSILON = 1e-06


def padded(cells, sides, width):
    for axis, dim in sides:
        count = lax.axis_size(axis)
        ends = count - 1
        head = lax.slice_in_dim(cells, 0, width, axis=dim)
        tail = lax.slice_in_dim(cells, cells.shape[dim] - width, cells.shape[dim], axis=dim)
        if count == 2:
            first = lax.axis_index(axis) == 0
            swapped = lax.ppermute(jnp.where(first, tail, head), axis, [(0, 1), (1, 0)])
            zeros = jnp.zeros_like(swapped)
            lower = jnp.where(first, zeros, swapped)
            upper = jnp.where(first, swapped, zeros)
        else:
            lower = lax.ppermute(tail, axis, [(i, (i + 1) % count) for i in range(ends)])
            upper = lax.ppermute(head, axis, [((i + 1) % count, i) for i in range(ends)])
        cells = jnp.concatenate([lower, cells, upper], axis=dim)
    return cells


def lag_table(first_bin):
    bin_number = first_bin + jnp.arange(BAND_BINS, dtype=jnp.int32)
    lag_number = jnp.arange(LAGS, dtype=jnp.int32) - LAGS // 2
    phase_steps = jnp.remainder(lag_number[:, None] * bin_number[None, :], 2 * BAND_BINS)
    phases = phase_steps.astype(jnp.float32) * (math.pi / BAND_BINS)
    normalizer = 1.0 / math.sqrt(SEGS * BAND_BINS)
    weights = jnp.stack([jnp.cos(phases), -jnp.sin(phases)], axis=2) * normalizer
    return weights.astype(jnp.bfloat16).reshape(LAGS, 2 * BAND_BINS)


def cross_terms(sources, receivers):
    src_real = sources[:, 0]
    src_imag = sources[:, 1]
    left_stack = jnp.stack(
        [jnp.concatenate([src_real, src_imag], 0), jnp.concatenate([src_imag, -src_real], 0)], 0
    )
    right_stack = jnp.concatenate([receivers[:, 0], receivers[:, 1]], 0)
    cross_spectra = jnp.einsum(
        "ctfs,tfn->fcsn", left_stack, right_stack, preferred_element_type=jnp.float32
    )
    return cross_spectra.astype(jnp.bfloat16)


def local(spectra, plan, pair_mask):
    seg_local = spectra.shape[0]
    band_bins = spectra.shape[2]
    sta_local = spectra.shape[3]
    band_position = lax.axis_index("band")
    sta_position = lax.axis_index("sta")
    seg_position = lax.axis_index("seg")
    total_bins = band_bins * lax.axis_size("band")
    half_sources = SRC // lax.axis_size("seg")
    amplitude = jnp.sqrt(spectra[:, 0] ** 2 + spectra[:, 1] ** 2)
    extended = padded(amplitude, (("band", 1),), HALF)
    block_width = 2 * HALF
    block_count = band_bins // block_width
    lower_part = extended[:, : block_count * block_width].reshape(
        seg_local, block_count, block_width, sta_local
    )
    upper_part = extended[:, block_width:].reshape(seg_local, block_count, block_width, sta_local)
    windows = jnp.concatenate([lower_part, upper_part], axis=2)
    offsets = jnp.arange(2 * block_width, dtype=jnp.int32)[:, None]
    targets = jnp.arange(block_width, dtype=jnp.int32)[None, :]
    band_matrix = ((offsets >= targets) & (offsets <= targets + 2 * HALF)).astype(jnp.float32)
    window_sums = jnp.einsum("tbgn,gf->tbfn", windows, band_matrix, precision=lax.Precision.HIGHEST)
    window_sums = window_sums.reshape(seg_local, band_bins, sta_local)
    bin_number = band_position * band_bins + jnp.arange(band_bins, dtype=jnp.int32)
    in_range = (
        jnp.minimum(bin_number + HALF, total_bins - 1) - jnp.maximum(bin_number - HALF, 0) + 1
    ).astype(jnp.float32)
    smooth = window_sums / in_range[None, :, None]
    white = (spectra / (smooth[:, None] + EPSILON)).astype(jnp.bfloat16)
    seg_count = lax.axis_size("seg")
    sta_count = lax.axis_size("sta")
    receivers = lax.all_gather(white, "seg", axis=0, tiled=True) if seg_count > 2 else None
    if receivers is None:
        partner = lax.ppermute(white, "seg", [(0, 1), (1, 0)])
        receivers = jnp.where(
            seg_position == 0,
            jnp.concatenate([white, partner], 0),
            jnp.concatenate([partner, white], 0),
        )
    own_half = lax.dynamic_slice_in_dim(receivers, seg_position * half_sources, half_sources, 3)
    shifted = [own_half]
    for shift in range(1, sta_count):
        shifted.append(
            lax.ppermute(own_half, "sta", [(i, (i + shift) % sta_count) for i in range(sta_count)])
        )
    candidates = jnp.stack(shifted, 0)
    plan, pair_mask, _ = lax.optimization_barrier((plan, pair_mask, own_half))
    steps_blocks = [plan[step_number] for step_number in range(STEPS)]
    mask_rows = [pair_mask[block].astype(jnp.float32) for block in steps_blocks]
    blk_dev = sta_local // SRC
    lag_weights = lag_table(band_position * band_bins).reshape(LAGS, band_bins, 2)
    receiver_ids = sta_position * sta_local + jnp.arange(sta_local, dtype=jnp.int32)
    block_columns = jnp.arange(pair_mask.shape[1], dtype=jnp.int32)
    block_onehot = ((receiver_ids // SRC)[:, None] == block_columns[None, :]).astype(jnp.float32)
    results = []
    for step_number in range(STEPS):
        block_number = steps_blocks[step_number]
        owner_position = block_number // blk_dev
        distance = (sta_position - owner_position) % sta_count
        held = lax.dynamic_index_in_dim(candidates, distance, 0, keepdims=False)
        sources = lax.dynamic_slice_in_dim(
            held, (block_number % blk_dev) * half_sources, half_sources, 3
        )
        cross_spectra = cross_terms(sources, receivers)
        correlated = lax.dot_general(
            lag_weights,
            cross_spectra,
            (((1, 2), (0, 1)), ((), ())),
            preferred_element_type=jnp.float32,
        )
        mask_row = mask_rows[step_number]
        allowed = jnp.sum(block_onehot * mask_row[None, :], axis=1)
        source_ids = (
            block_number * SRC
            + seg_position * half_sources
            + jnp.arange(half_sources, dtype=jnp.int32)
        )
        keep_pairs = (source_ids[:, None] != receiver_ids[None, :]).astype(jnp.float32) * allowed[
            None, :
        ]
        results.append((correlated * keep_pairs[None]).astype(jnp.bfloat16))
    return jnp.stack(results, 0)


def solution(mesh):
    return jax.shard_map(
        local,
        mesh=mesh,
        in_specs=(P("seg", None, "band", ("groups", "sta")), P("groups"), P("groups", None)),
        out_specs=P(None, "band", "seg", ("groups", "sta")),
        check_vma=False,
    )
```

```python
import math

import jax
import jax.numpy as jnp
from jax import lax
from jax.sharding import PartitionSpec as P


SEGS = 8
STEPS = 2
SRC = 128
BAND_BINS = 256
HALF = 64
LAGS = 128


EPSILON = 1e-06


def padded(cells, sides, width):
    for axis, dim in sides:
        count = lax.axis_size(axis)
        ends = count - 1
        head = lax.slice_in_dim(cells, 0, width, axis=dim)
        tail = lax.slice_in_dim(cells, cells.shape[dim] - width, cells.shape[dim], axis=dim)
        if count == 2:
            first = lax.axis_index(axis) == 0
            swapped = lax.ppermute(jnp.where(first, tail, head), axis, [(0, 1), (1, 0)])
            zeros = jnp.zeros_like(swapped)
            lower = jnp.where(first, zeros, swapped)
            upper = jnp.where(first, swapped, zeros)
        else:
            lower = lax.ppermute(tail, axis, [(i, (i + 1) % count) for i in range(ends)])
            upper = lax.ppermute(head, axis, [((i + 1) % count, i) for i in range(ends)])
        cells = jnp.concatenate([lower, cells, upper], axis=dim)
    return cells


def lag_table(first_bin):
    bin_number = first_bin + jnp.arange(BAND_BINS, dtype=jnp.int32)
    lag_number = jnp.arange(LAGS, dtype=jnp.int32) - LAGS // 2
    phase_steps = jnp.remainder(lag_number[:, None] * bin_number[None, :], 2 * BAND_BINS)
    phases = phase_steps.astype(jnp.float32) * (math.pi / BAND_BINS)
    normalizer = 1.0 / math.sqrt(SEGS * BAND_BINS)
    weights = jnp.stack([jnp.cos(phases), -jnp.sin(phases)], axis=2) * normalizer
    return weights.astype(jnp.bfloat16).reshape(LAGS, 2 * BAND_BINS)


def cross_terms(sources, receivers):
    src_real = sources[:, 0]
    src_imag = sources[:, 1]
    left_stack = jnp.stack(
        [jnp.concatenate([src_real, src_imag], 0), jnp.concatenate([src_imag, -src_real], 0)], 0
    )
    right_stack = jnp.concatenate([receivers[:, 0], receivers[:, 1]], 0)
    cross_spectra = jnp.einsum(
        "ctfs,tfn->fcsn", left_stack, right_stack, preferred_element_type=jnp.float32
    )
    return cross_spectra.astype(jnp.bfloat16)


def local(spectra, plan, pair_mask):
    seg_local = spectra.shape[0]
    band_bins = spectra.shape[2]
    sta_local = spectra.shape[3]
    band_position = lax.axis_index("band")
    sta_position = lax.axis_index("sta")
    seg_position = lax.axis_index("seg")
    total_bins = band_bins * lax.axis_size("band")
    half_sources = SRC // lax.axis_size("seg")
    amplitude = jnp.sqrt(spectra[:, 0] ** 2 + spectra[:, 1] ** 2)
    extended = padded(amplitude, (("band", 1),), HALF)
    block_width = 2 * HALF
    block_count = band_bins // block_width
    lower_part = extended[:, : block_count * block_width].reshape(
        seg_local, block_count, block_width, sta_local
    )
    upper_part = extended[:, block_width:].reshape(seg_local, block_count, block_width, sta_local)
    windows = jnp.concatenate([lower_part, upper_part], axis=2)
    offsets = jnp.arange(2 * block_width, dtype=jnp.int32)[:, None]
    targets = jnp.arange(block_width, dtype=jnp.int32)[None, :]
    band_matrix = ((offsets >= targets) & (offsets <= targets + 2 * HALF)).astype(jnp.float32)
    window_sums = jnp.einsum("tbgn,gf->tbfn", windows, band_matrix, precision=lax.Precision.HIGHEST)
    window_sums = window_sums.reshape(seg_local, band_bins, sta_local)
    bin_number = band_position * band_bins + jnp.arange(band_bins, dtype=jnp.int32)
    in_range = (
        jnp.minimum(bin_number + HALF, total_bins - 1) - jnp.maximum(bin_number - HALF, 0) + 1
    ).astype(jnp.float32)
    smooth = window_sums / in_range[None, :, None]
    white = (spectra / (smooth[:, None] + EPSILON)).astype(jnp.bfloat16)
    seg_count = lax.axis_size("seg")
    sta_count = lax.axis_size("sta")
    receivers = lax.all_gather(white, "seg", axis=0, tiled=True) if seg_count > 2 else None
    if receivers is None:
        partner = lax.ppermute(white, "seg", [(0, 1), (1, 0)])
        receivers = jnp.concatenate([white, partner], 0)
    own_half = lax.dynamic_slice_in_dim(receivers, seg_position * half_sources, half_sources, 3)
    shifted = [own_half]
    for shift in range(1, sta_count):
        shifted.append(
            lax.ppermute(own_half, "sta", [(i, (i + shift) % sta_count) for i in range(sta_count)])
        )
    candidates = jnp.stack(shifted, 0)
    plan, pair_mask, _ = lax.optimization_barrier((plan, pair_mask, own_half))
    steps_blocks = [plan[step_number] for step_number in range(STEPS)]
    mask_rows = [pair_mask[block].astype(jnp.float32) for block in steps_blocks]
    blk_dev = sta_local // SRC
    lag_weights = lag_table(band_position * band_bins).reshape(LAGS, band_bins, 2)
    receiver_ids = sta_position * sta_local + jnp.arange(sta_local, dtype=jnp.int32)
    block_columns = jnp.arange(pair_mask.shape[1], dtype=jnp.int32)
    block_onehot = ((receiver_ids // SRC)[:, None] == block_columns[None, :]).astype(jnp.float32)
    results = []
    for step_number in range(STEPS):
        block_number = steps_blocks[step_number]
        owner_position = block_number // blk_dev
        distance = (sta_position - owner_position) % sta_count
        held = lax.dynamic_index_in_dim(candidates, distance, 0, keepdims=False)
        sources = lax.dynamic_slice_in_dim(
            held, (block_number % blk_dev) * half_sources, half_sources, 3
        )
        cross_spectra = cross_terms(sources, receivers)
        correlated = lax.dot_general(
            lag_weights,
            cross_spectra,
            (((1, 2), (0, 1)), ((), ())),
            preferred_element_type=jnp.float32,
        )
        mask_row = mask_rows[step_number]
        allowed = jnp.sum(block_onehot * mask_row[None, :], axis=1)
        source_ids = (
            block_number * SRC
            + seg_position * half_sources
            + jnp.arange(half_sources, dtype=jnp.int32)
        )
        keep_pairs = (source_ids[:, None] != receiver_ids[None, :]).astype(jnp.float32) * allowed[
            None, :
        ]
        results.append((correlated * keep_pairs[None]).astype(jnp.bfloat16))
    return jnp.stack(results, 0)


def solution(mesh):
    return jax.shard_map(
        local,
        mesh=mesh,
        in_specs=(P("seg", None, "band", ("groups", "sta")), P("groups"), P("groups", None)),
        out_specs=P(None, "band", "seg", ("groups", "sta")),
        check_vma=False,
    )
```

```python
import math

import jax
import jax.numpy as jnp
from jax import lax
from jax.sharding import PartitionSpec as P


SEGS = 8
STEPS = 2
SRC = 128
BAND_BINS = 256
HALF = 64
LAGS = 128


EPSILON = 1e-06


def padded(cells, sides, width):
    for axis, dim in sides:
        count = lax.axis_size(axis)
        ends = count - 1
        head = lax.slice_in_dim(cells, 0, width, axis=dim)
        tail = lax.slice_in_dim(cells, cells.shape[dim] - width, cells.shape[dim], axis=dim)
        if count == 2:
            first = lax.axis_index(axis) == 0
            swapped = lax.ppermute(jnp.where(first, tail, head), axis, [(0, 1), (1, 0)])
            zeros = jnp.zeros_like(swapped)
            lower = jnp.where(first, zeros, swapped)
            upper = jnp.where(first, swapped, zeros)
        else:
            lower = lax.ppermute(tail, axis, [(i, (i + 1) % count) for i in range(ends)])
            upper = lax.ppermute(head, axis, [((i + 1) % count, i) for i in range(ends)])
        cells = jnp.concatenate([lower, cells, upper], axis=dim)
    return cells


def lag_table(first_bin):
    bin_number = first_bin + jnp.arange(BAND_BINS, dtype=jnp.int32)
    lag_number = jnp.arange(LAGS, dtype=jnp.int32) - LAGS // 2
    phase_steps = jnp.remainder(lag_number[:, None] * bin_number[None, :], 2 * BAND_BINS)
    phases = phase_steps.astype(jnp.float32) * (math.pi / BAND_BINS)
    normalizer = 1.0 / math.sqrt(SEGS * BAND_BINS)
    weights = jnp.stack([jnp.cos(phases), -jnp.sin(phases)], axis=2) * normalizer
    return weights.astype(jnp.bfloat16).reshape(LAGS, 2 * BAND_BINS)


def cross_terms(sources, receivers):
    src_real = sources[:, 0]
    src_imag = sources[:, 1]
    left_stack = jnp.stack(
        [jnp.concatenate([src_real, src_imag], 0), jnp.concatenate([src_imag, -src_real], 0)], 0
    )
    right_stack = jnp.concatenate([receivers[:, 0], receivers[:, 1]], 0)
    cross_spectra = jnp.einsum(
        "ctfs,tfn->fcsn", left_stack, right_stack, preferred_element_type=jnp.float32
    )
    return cross_spectra.astype(jnp.bfloat16)


def local(spectra, plan, pair_mask):
    seg_local = spectra.shape[0]
    band_bins = spectra.shape[2]
    sta_local = spectra.shape[3]
    band_position = lax.axis_index("band")
    sta_position = lax.axis_index("sta")
    seg_position = lax.axis_index("seg")
    total_bins = band_bins * lax.axis_size("band")
    half_sources = SRC // lax.axis_size("seg")
    if lax.axis_size("band") == 2:
        first = band_position == 0
        edge = lax.dynamic_slice_in_dim(
            spectra, (1 - band_position) * (band_bins - HALF), HALF, 2
        )
        edge_amplitude = jnp.sqrt(edge[:, 0] ** 2 + edge[:, 1] ** 2)
        swapped = lax.ppermute(edge_amplitude, "band", [(0, 1), (1, 0)])
        held, _ = lax.optimization_barrier((spectra, edge_amplitude))
        amplitude = jnp.sqrt(held[:, 0] ** 2 + held[:, 1] ** 2)
        zeros = jnp.zeros_like(swapped)
        extended = jnp.concatenate(
            [jnp.where(first, zeros, swapped), amplitude, jnp.where(first, swapped, zeros)], 1
        )
    else:
        amplitude = jnp.sqrt(spectra[:, 0] ** 2 + spectra[:, 1] ** 2)
        extended = padded(amplitude, (("band", 1),), HALF)
    block_width = 2 * HALF
    block_count = band_bins // block_width
    lower_part = extended[:, : block_count * block_width].reshape(
        seg_local, block_count, block_width, sta_local
    )
    upper_part = extended[:, block_width:].reshape(seg_local, block_count, block_width, sta_local)
    windows = jnp.concatenate([lower_part, upper_part], axis=2)
    offsets = jnp.arange(2 * block_width, dtype=jnp.int32)[:, None]
    targets = jnp.arange(block_width, dtype=jnp.int32)[None, :]
    band_matrix = ((offsets >= targets) & (offsets <= targets + 2 * HALF)).astype(jnp.float32)
    window_sums = jnp.einsum("tbgn,gf->tbfn", windows, band_matrix, precision=lax.Precision.HIGHEST)
    window_sums = window_sums.reshape(seg_local, band_bins, sta_local)
    bin_number = band_position * band_bins + jnp.arange(band_bins, dtype=jnp.int32)
    in_range = (
        jnp.minimum(bin_number + HALF, total_bins - 1) - jnp.maximum(bin_number - HALF, 0) + 1
    ).astype(jnp.float32)
    smooth = window_sums / in_range[None, :, None]
    white = (spectra / (smooth[:, None] + EPSILON)).astype(jnp.bfloat16)
    seg_count = lax.axis_size("seg")
    sta_count = lax.axis_size("sta")
    receivers = lax.all_gather(white, "seg", axis=0, tiled=True) if seg_count > 2 else None
    if receivers is None:
        partner = lax.ppermute(white, "seg", [(0, 1), (1, 0)])
        receivers = jnp.where(
            seg_position == 0,
            jnp.concatenate([white, partner], 0),
            jnp.concatenate([partner, white], 0),
        )
    own_half = lax.dynamic_slice_in_dim(receivers, seg_position * half_sources, half_sources, 3)
    shifted = [own_half]
    for shift in range(1, sta_count):
        shifted.append(
            lax.ppermute(own_half, "sta", [(i, (i + shift) % sta_count) for i in range(sta_count)])
        )
    candidates = jnp.stack(shifted, 0)
    plan, pair_mask, _ = lax.optimization_barrier((plan, pair_mask, own_half))
    steps_blocks = [plan[step_number] for step_number in range(STEPS)]
    mask_rows = [pair_mask[block].astype(jnp.float32) for block in steps_blocks]
    blk_dev = sta_local // SRC
    lag_weights = lag_table(band_position * band_bins).reshape(LAGS, band_bins, 2)
    receiver_ids = sta_position * sta_local + jnp.arange(sta_local, dtype=jnp.int32)
    block_columns = jnp.arange(pair_mask.shape[1], dtype=jnp.int32)
    block_onehot = ((receiver_ids // SRC)[:, None] == block_columns[None, :]).astype(jnp.float32)
    results = []
    for step_number in range(STEPS):
        block_number = steps_blocks[step_number]
        owner_position = block_number // blk_dev
        distance = (sta_position - owner_position) % sta_count
        held = lax.dynamic_index_in_dim(candidates, distance, 0, keepdims=False)
        sources = lax.dynamic_slice_in_dim(
            held, (block_number % blk_dev) * half_sources, half_sources, 3
        )
        cross_spectra = cross_terms(sources, receivers)
        correlated = lax.dot_general(
            lag_weights,
            cross_spectra,
            (((1, 2), (0, 1)), ((), ())),
            preferred_element_type=jnp.float32,
        )
        mask_row = mask_rows[step_number]
        allowed = jnp.sum(block_onehot * mask_row[None, :], axis=1)
        source_ids = (
            block_number * SRC
            + seg_position * half_sources
            + jnp.arange(half_sources, dtype=jnp.int32)
        )
        keep_pairs = (source_ids[:, None] != receiver_ids[None, :]).astype(jnp.float32) * allowed[
            None, :
        ]
        results.append((correlated * keep_pairs[None]).astype(jnp.bfloat16))
    return jnp.stack(results, 0)


def solution(mesh):
    return jax.shard_map(
        local,
        mesh=mesh,
        in_specs=(P("seg", None, "band", ("groups", "sta")), P("groups"), P("groups", None)),
        out_specs=P(None, "band", "seg", ("groups", "sta")),
        check_vma=False,
    )
```

```python
import math

import jax
import jax.numpy as jnp
from jax import lax
from jax.sharding import PartitionSpec as P


SEGS = 8
STEPS = 2
SRC = 128
BAND_BINS = 256
HALF = 64
LAGS = 128


EPSILON = 1e-06


def padded(cells, sides, width):
    for axis, dim in sides:
        count = lax.axis_size(axis)
        ends = count - 1
        head = lax.slice_in_dim(cells, 0, width, axis=dim)
        tail = lax.slice_in_dim(cells, cells.shape[dim] - width, cells.shape[dim], axis=dim)
        if count == 2:
            first = lax.axis_index(axis) == 0
            swapped = lax.ppermute(jnp.where(first, tail, head), axis, [(0, 1), (1, 0)])
            zeros = jnp.zeros_like(swapped)
            lower = jnp.where(first, zeros, swapped)
            upper = jnp.where(first, swapped, zeros)
        else:
            lower = lax.ppermute(tail, axis, [(i, (i + 1) % count) for i in range(ends)])
            upper = lax.ppermute(head, axis, [((i + 1) % count, i) for i in range(ends)])
        cells = jnp.concatenate([lower, cells, upper], axis=dim)
    return cells


def lag_table(first_bin):
    bin_number = first_bin + jnp.arange(BAND_BINS, dtype=jnp.int32)
    lag_number = jnp.arange(LAGS, dtype=jnp.int32) - LAGS // 2
    phase_steps = jnp.remainder(lag_number[:, None] * bin_number[None, :], 2 * BAND_BINS)
    phases = phase_steps.astype(jnp.float32) * (math.pi / BAND_BINS)
    normalizer = 1.0 / math.sqrt(SEGS * BAND_BINS)
    weights = jnp.stack([jnp.cos(phases), -jnp.sin(phases)], axis=2) * normalizer
    return weights.astype(jnp.bfloat16).reshape(LAGS, 2 * BAND_BINS)


def cross_terms(sources, receivers):
    src_real = sources[:, 0]
    src_imag = sources[:, 1]
    left_stack = jnp.stack(
        [jnp.concatenate([src_real, src_imag], 0), jnp.concatenate([src_imag, -src_real], 0)], 0
    )
    right_stack = jnp.concatenate([receivers[:, 0], receivers[:, 1]], 0)
    cross_spectra = jnp.einsum(
        "ctfs,tfn->fcsn", left_stack, right_stack, preferred_element_type=jnp.float32
    )
    return cross_spectra.astype(jnp.bfloat16)


def local(spectra, plan, pair_mask):
    seg_local = spectra.shape[0]
    band_bins = spectra.shape[2]
    sta_local = spectra.shape[3]
    band_position = lax.axis_index("band")
    sta_position = lax.axis_index("sta")
    seg_position = lax.axis_index("seg")
    total_bins = band_bins * lax.axis_size("band")
    half_sources = SRC // lax.axis_size("seg")
    if lax.axis_size("band") == 2:
        first = band_position == 0
        edge = jnp.where(first, spectra[:, :, band_bins - HALF :], spectra[:, :, :HALF])
        edge_amplitude = jnp.sqrt(edge[:, 0] ** 2 + edge[:, 1] ** 2)
        swapped = lax.ppermute(edge_amplitude, "band", [(0, 1), (1, 0)])
        held, _ = lax.optimization_barrier((spectra, edge_amplitude))
        amplitude = jnp.sqrt(held[:, 0] ** 2 + held[:, 1] ** 2)
        zeros = jnp.zeros_like(swapped)
        extended = jnp.concatenate(
            [jnp.where(first, zeros, swapped), amplitude, jnp.where(first, swapped, zeros)], 1
        )
    else:
        amplitude = jnp.sqrt(spectra[:, 0] ** 2 + spectra[:, 1] ** 2)
        extended = padded(amplitude, (("band", 1),), HALF)
    block_width = 2 * HALF
    block_count = band_bins // block_width
    lower_part = extended[:, : block_count * block_width].reshape(
        seg_local, block_count, block_width, sta_local
    )
    upper_part = extended[:, block_width:].reshape(seg_local, block_count, block_width, sta_local)
    windows = jnp.concatenate([lower_part, upper_part], axis=2)
    offsets = jnp.arange(2 * block_width, dtype=jnp.int32)[:, None]
    targets = jnp.arange(block_width, dtype=jnp.int32)[None, :]
    band_matrix = ((offsets >= targets) & (offsets <= targets + 2 * HALF)).astype(jnp.float32)
    window_sums = jnp.einsum("tbgn,gf->tbfn", windows, band_matrix, precision=lax.Precision.HIGHEST)
    window_sums = window_sums.reshape(seg_local, band_bins, sta_local)
    bin_number = band_position * band_bins + jnp.arange(band_bins, dtype=jnp.int32)
    in_range = (
        jnp.minimum(bin_number + HALF, total_bins - 1) - jnp.maximum(bin_number - HALF, 0) + 1
    ).astype(jnp.float32)
    smooth = window_sums / in_range[None, :, None]
    white = (spectra / (smooth[:, None] + EPSILON)).astype(jnp.bfloat16)
    seg_count = lax.axis_size("seg")
    sta_count = lax.axis_size("sta")
    receivers = lax.all_gather(white, "seg", axis=0, tiled=True) if seg_count > 2 else None
    if receivers is None:
        partner = lax.ppermute(white, "seg", [(0, 1), (1, 0)])
        receivers = jnp.where(
            seg_position == 0,
            jnp.concatenate([white, partner], 0),
            jnp.concatenate([partner, white], 0),
        )
    own_half = lax.dynamic_slice_in_dim(receivers, seg_position * half_sources, half_sources, 3)
    shifted = [own_half]
    for shift in range(1, sta_count):
        shifted.append(
            lax.ppermute(own_half, "sta", [(i, (i + shift) % sta_count) for i in range(sta_count)])
        )
    plan, pair_mask, _ = lax.optimization_barrier((plan, pair_mask, own_half))
    steps_blocks = [plan[step_number] for step_number in range(STEPS)]
    mask_rows = [pair_mask[block].astype(jnp.float32) for block in steps_blocks]
    blk_dev = sta_local // SRC
    lag_weights = lag_table(band_position * band_bins).reshape(LAGS, band_bins, 2)
    receiver_ids = sta_position * sta_local + jnp.arange(sta_local, dtype=jnp.int32)
    block_columns = jnp.arange(pair_mask.shape[1], dtype=jnp.int32)
    block_onehot = ((receiver_ids // SRC)[:, None] == block_columns[None, :]).astype(jnp.float32)
    results = []
    for step_number in range(STEPS):
        block_number = steps_blocks[step_number]
        owner_position = block_number // blk_dev
        distance = (sta_position - owner_position) % sta_count
        held = shifted[0]
        for shift in range(1, sta_count):
            held = jnp.where(distance == shift, shifted[shift], held)
        sources = lax.dynamic_slice_in_dim(
            held, (block_number % blk_dev) * half_sources, half_sources, 3
        )
        cross_spectra = cross_terms(sources, receivers)
        correlated = lax.dot_general(
            lag_weights,
            cross_spectra,
            (((1, 2), (0, 1)), ((), ())),
            preferred_element_type=jnp.float32,
        )
        mask_row = mask_rows[step_number]
        allowed = jnp.sum(block_onehot * mask_row[None, :], axis=1)
        source_ids = (
            block_number * SRC
            + seg_position * half_sources
            + jnp.arange(half_sources, dtype=jnp.int32)
        )
        keep_pairs = (source_ids[:, None] != receiver_ids[None, :]).astype(jnp.float32) * allowed[
            None, :
        ]
        results.append((correlated * keep_pairs[None]).astype(jnp.bfloat16))
    return jnp.stack(results, 0)


def solution(mesh):
    return jax.shard_map(
        local,
        mesh=mesh,
        in_specs=(P("seg", None, "band", ("groups", "sta")), P("groups"), P("groups", None)),
        out_specs=P(None, "band", "seg", ("groups", "sta")),
        check_vma=False,
    )
```
